256 devices in a mesh: ctx: 64 (over y, z, core), head: 4 (over x).
Axes of the slice: x: 4, y: 4, z: 8, core: 2. Of those that a mesh axis runs over, the one named last changes fastest.
Arguments:
- linear_query: bfloat16 [16384, 8192], P('ctx', 'head'), may hold values from -6 to 6
- linear_key: bfloat16 [16384, 8192], P('ctx', 'head'), may hold values from -6 to 6
- linear_value: bfloat16 [16384, 8192], P('ctx', 'head'), may hold values from -6 to 6
- log_decay: float32 [64, 16384], P('head', 'ctx'), may hold values from -1.2 to 0, as said below
- norm_gain: float32 [8192], P('head'), may hold values from 0.25 to 1.75
- soft_query: bfloat16 [16384, 8192], P('ctx', 'head'), may hold values from -4.5 to 4.5
- soft_key: bfloat16 [16384, 8192], P('ctx', 'head'), may hold values from -4.5 to 4.5
- soft_value: bfloat16 [16384, 8192], P('ctx', 'head'), may hold values from -6 to 6
- block_index: int32 [128, 5], P('ctx'), may hold values from 0 to 127, as said below
- block_count: int32 [128], P('ctx'), may hold values from 1 to 5, as said below
Outputs:
- linear_rows: bfloat16 [16384, 8192], P(('ctx', 'head'))
- softmax_rows: bfloat16 [16384, 8192], P(('ctx', 'head'))
The draws below stay inside these ranges and needn't reach their ends.
Inputs may be any that keep to these rules, and one draw needn't show every extreme that they name: `block_index`: entry 0 of row r is r itself; entries 1 to block_count[r] - 1 are distinct blocks from r - 4 to r - 1, and the farthest of them, r - 4, is named in some row; the entries from block_count[r] on equal r. `block_count`: at most r + 1 for row r; 5 in some row. `log_decay`: strictly negative.
All inputs are finite; a program needn't handle non-finite values.
Results may differ from the reference program's by a relative error of at most 0.0057.
Values may be sent and summed in bfloat16 or wider, within the bound.
No kernel may reach another device: no remote copies, remote signals or barrier semaphores. Data moves between devices by JAX's collectives and lax.ppermute only.
A program may use at most 192 MiB of HBM per device.

```python
import math
import jax
import jax.numpy as jnp
from jax import lax

H = 64
HD = 128
SEC = 256
BLK = 128
KMAX = 5
WIN_SEC = 2
CONTEXT_TOKENS = 16384
QBLOCKS = 128


def draw_log_decay(key, part):
    every_key = jax.random.split(key, 7)
    fast_share = 50
    heads_fast = jax.random.randint(every_key[0], (H,), 0, 100) < fast_share
    fast_rate = jnp.exp(jax.random.uniform(every_key[1], (H,), minval=math.log(1.0 / 50.0), maxval=math.log(1.0 / 25.0)))
    slow_rate = jnp.exp(jax.random.uniform(every_key[2], (H,), minval=0.0, maxval=math.log(2.0))) * (0.2 / CONTEXT_TOKENS)
    baseline_rate = jnp.where(heads_fast, fast_rate, slow_rate)
    sections = CONTEXT_TOKENS // SEC
    section_factor = jnp.exp(jax.random.uniform(every_key[3], (H, sections), minval=math.log(0.5), maxval=math.log(2.0)))
    quiet_sections = jax.random.bernoulli(jax.random.fold_in(key, 9), 0.5, (H, sections))
    section_factor = jnp.where(heads_fast[:, None] & quiet_sections, section_factor * 0.005, section_factor)
    token_multiplier = jnp.repeat(section_factor, SEC, axis=1)
    jaggedness = jax.random.uniform(every_key[4], (H, CONTEXT_TOKENS), minval=0.5, maxval=1.5)
    spike_locations = jax.random.randint(every_key[5], (2,), 0, CONTEXT_TOKENS)
    spike_depth = jnp.log(jax.random.uniform(every_key[6], (2,), minval=0.6, maxval=0.8))
    token_positions = jnp.arange(CONTEXT_TOKENS, dtype=jnp.int32)
    spike_events = jnp.sum(jnp.where(token_positions[None, :] == spike_locations[:, None], spike_depth[:, None], 0.0), axis=0)
    return (-baseline_rate[:, None] * token_multiplier * jaggedness + spike_events[None, :]).astype(jnp.float32)


def drawn_field(key):
    return jax.random.truncated_normal(key, -4.5, 4.5, (CONTEXT_TOKENS, H * HD))


def draw_soft_key(key, part):
    values_drawn = drawn_field(jax.random.fold_in(key, 1)).reshape(QBLOCKS, BLK, H, HD)
    return values_drawn.reshape(CONTEXT_TOKENS, H * HD).astype(jnp.bfloat16)


def draw_soft_query(key, part):
    values_drawn = drawn_field(jax.random.fold_in(key, 2)).reshape(QBLOCKS, BLK, H, HD)
    return values_drawn.reshape(CONTEXT_TOKENS, H * HD).astype(jnp.bfloat16)


def pattern_tables(key):
    base = jax.random.fold_in(key, 11)
    key_floor, key_count, key_order = jax.random.split(base, 3)
    per_section = SEC // BLK
    span = WIN_SEC * per_section
    rows_all = jnp.arange(QBLOCKS, dtype=jnp.int32)
    floors = jnp.repeat(jax.random.randint(key_floor, (QBLOCKS // per_section,), 1, KMAX + 1), per_section)
    counts = jax.random.randint(key_count, (QBLOCKS,), floors, KMAX + 1)
    counts = jnp.minimum(counts, rows_all + 1)
    is_last = rows_all == QBLOCKS - 1
    counts = jnp.where(is_last, KMAX, counts)
    orders = jax.vmap(lambda subkey: jax.random.permutation(subkey, span))(jax.random.split(key_order, QBLOCKS))
    offsets = jnp.arange(1, span + 1, dtype=jnp.int32)
    beyond = (offsets[None, :] > rows_all[:, None]).astype(jnp.int32)
    farthest = (is_last[:, None] & (offsets[None, :] == span)).astype(jnp.int32)
    scores = orders.astype(jnp.int32) + span * beyond - 2 * span * farthest
    chosen = jnp.argsort(scores, axis=1, stable=True)[:, :KMAX - 1].astype(jnp.int32) + 1
    others = rows_all[:, None] - chosen
    slots = jnp.arange(1, KMAX, dtype=jnp.int32)
    others = jnp.where(slots[None, :] < counts[:, None], others, rows_all[:, None])
    index = jnp.concatenate([rows_all[:, None], others], axis=1)
    return (index.astype(jnp.int32), counts.astype(jnp.int32))


def draw_block_index(key, part):
    return pattern_tables(key)[0]


def draw_block_count(key, part):
    return pattern_tables(key)[1]


def block_scale(rng, dims, cuts, smallest, high):
    level, own = 1.0, jax.random.fold_in(rng, 6)
    for dim, blocks in cuts:
        steps = jnp.exp(jax.random.uniform(jax.random.fold_in(own, dim), (blocks,), jnp.float32, smallest / len(cuts), high / len(cuts)))
        level = level * jnp.repeat(steps, dims[dim] // blocks).reshape([-1 if axis == dim else 1 for axis in range(len(dims))])
    return level


def centred(own_key, extent, deviation, most, cuts=(), held_as=jnp.bfloat16):
    result = jax.random.normal(own_key, extent, jnp.float32) * deviation
    if len(cuts) > 0:
        result = block_scale(own_key, extent, cuts, -0.22, 0.18) * result
    return jnp.clip(result, min=-most, max=most).astype(held_as)


def setup_inputs(seed: int = 0) -> dict:
    key_list = jax.random.split(jax.random.key(seed), 11)
    return {
        "linear_query": centred(key_list[0], (CONTEXT_TOKENS, H * HD), 1.0, 6.0, ((0, 64), (1, 4))),
        "linear_key": centred(key_list[1], (CONTEXT_TOKENS, H * HD), 1.0, 6.0, ((0, 64), (1, 4))),
        "linear_value": centred(key_list[2], (CONTEXT_TOKENS, H * HD), 1.0, 6.0, ((0, 64), (1, 4))),
        "log_decay": draw_log_decay(jax.random.fold_in(key_list[10], 71), 0),
        "norm_gain": jnp.clip(1.0 + 0.15 * jax.random.normal(key_list[4], (H * HD,), jnp.float32), 0.25, 1.75),
        "soft_query": draw_soft_query(jax.random.fold_in(key_list[10], 71), 0),
        "soft_key": draw_soft_key(jax.random.fold_in(key_list[10], 71), 0),
        "soft_value": centred(key_list[7], (CONTEXT_TOKENS, H * HD), 1.0, 6.0, ((0, 64), (1, 4))),
        "block_index": draw_block_index(jax.random.fold_in(key_list[10], 71), 0),
        "block_count": draw_block_count(jax.random.fold_in(key_list[10], 71), 0),
    }


EPS = 1e-06

def rounded(matrix):
    return lax.optimization_barrier(matrix.astype(jnp.bfloat16)).astype(jnp.float32)

def causal_mask(length):
    rows_iota = lax.broadcasted_iota(jnp.int32, (length, length), 0)
    cols_iota = lax.broadcasted_iota(jnp.int32, (length, length), 1)
    return cols_iota <= rows_iota

def block_decays(decay_sec):
    per_block = decay_sec.reshape(H, SEC // BLK, BLK).transpose(1, 0, 2)
    cumulative = jnp.cumsum(per_block, axis=2)
    return (cumulative, cumulative[:, :, -1])

def state_step(carried, keys_blk, values_blk, cumul_blk, total_blk):
    keys_wide = keys_blk.astype(jnp.float32)
    values_wide = values_blk.astype(jnp.float32)
    decayed = rounded(keys_wide * jnp.exp(total_blk[:, None] - cumul_blk).T[:, :, None])
    update = jnp.einsum('jhd,jhe->hde', decayed, values_wide)
    return jnp.exp(total_blk)[:, None, None] * carried + update

def section_states(inputs):
    key_sec, value_sec, decay_sec = inputs
    cumulative, totals = block_decays(decay_sec)
    keys_blocks = key_sec.reshape(SEC // BLK, BLK, H, HD)
    values_blocks = value_sec.reshape(SEC // BLK, BLK, H, HD)

    def advance(carried, pieces):
        return (state_step(carried, pieces[0], pieces[1], pieces[2], pieces[3]), 0.0)
    start = jnp.zeros((H, HD, HD), jnp.float32)
    final, unused = lax.scan(advance, start, (keys_blocks, values_blocks, cumulative, totals))
    return (final, lax.optimization_barrier(jnp.sum(decay_sec, axis=1)))

def section_output(inputs):
    query_sec, key_sec, value_sec, decay_sec, incoming, gain = inputs
    cumulative, totals = block_decays(decay_sec)
    query_blocks = query_sec.reshape(SEC // BLK, BLK, H, HD)
    keys_blocks = key_sec.reshape(SEC // BLK, BLK, H, HD)
    values_blocks = value_sec.reshape(SEC // BLK, BLK, H, HD)
    allowed = causal_mask(BLK)

    def advance(carried, pieces):
        query_blk, keys_blk, values_blk, cumul_blk, total_blk = pieces
        query_wide = query_blk.astype(jnp.float32)
        scores = jnp.einsum('thd,jhd->htj', query_wide, keys_blk.astype(jnp.float32))
        differ = cumul_blk[:, :, None] - cumul_blk[:, None, :]
        weights = jnp.where(allowed[None], jnp.exp(jnp.minimum(differ, 0.0)), 0.0)
        inside = jnp.einsum('htj,jhd->thd', rounded(scores * weights), values_blk.astype(jnp.float32))
        decayed_query = rounded(query_wide * jnp.exp(cumul_blk).T[:, :, None])
        across = jnp.einsum('thd,hde->the', decayed_query, rounded(carried))
        following = state_step(carried, keys_blk, values_blk, cumul_blk, total_blk)
        return (following, inside + across)
    start = jnp.zeros((H, HD, HD), jnp.float32)
    final, outputs = lax.scan(advance, start, (query_blocks, keys_blocks, values_blocks, cumulative, totals))
    section_cum = jnp.cumsum(decay_sec, axis=1)
    scaled = rounded(query_sec.astype(jnp.float32) * jnp.exp(section_cum).T[:, :, None])
    raw = outputs.reshape(SEC, H, HD) + jnp.einsum('thd,hde->the', scaled, rounded(incoming))
    square_mean = lax.optimization_barrier(jnp.mean(raw * raw, axis=2, keepdims=True))
    normed = raw / jnp.sqrt(square_mean + EPS) * gain.reshape(H, HD)
    return normed.astype(jnp.bfloat16).reshape(SEC, H * HD)

def attend(query_blk, keys_sel, values_sel, index_row, count_row, row_global):
    inverse_root = 1.0 / math.sqrt(HD)
    scores = jnp.einsum('thd,kjhd->htkj', query_blk.astype(jnp.float32), keys_sel.astype(jnp.float32)) * inverse_root
    slot_used = jnp.arange(index_row.shape[0], dtype=jnp.int32) < count_row
    off_diagonal = jnp.logical_not(index_row == row_global)
    allowed = slot_used[None, :, None] & (off_diagonal[None, :, None] | causal_mask(BLK)[:, None, :])
    scores = jnp.where(allowed[None], scores, -jnp.inf)
    highest = lax.optimization_barrier(jnp.max(scores, axis=(2, 3), keepdims=True))
    raised = jnp.exp(scores - highest)
    weights = rounded(raised / lax.optimization_barrier(jnp.sum(raised, axis=(2, 3), keepdims=True)))
    output = jnp.einsum('htkj,kjhd->thd', weights, values_sel.astype(jnp.float32))
    return output.astype(jnp.bfloat16).reshape(BLK, H * HD)

def reference(linear_query, linear_key, linear_value, log_decay, norm_gain, soft_query, soft_key, soft_value, block_index, block_count):
    sections = CONTEXT_TOKENS // SEC
    query_secs = linear_query.reshape(sections, SEC, H, HD)
    key_secs = linear_key.reshape(sections, SEC, H, HD)
    value_secs = linear_value.reshape(sections, SEC, H, HD)
    decay_secs = log_decay.reshape(H, sections, SEC).transpose(1, 0, 2)
    finals, totals = lax.map(section_states, (key_secs, value_secs, decay_secs))

    def chained(carried, pieces):
        return (jnp.exp(pieces[1])[:, None, None] * carried + pieces[0], carried)
    last_state, incoming = lax.scan(chained, jnp.zeros((H, HD, HD), jnp.float32), (finals, totals))
    gains = jnp.broadcast_to(norm_gain, (sections, H * HD))
    linear_out = lax.map(section_output, (query_secs, key_secs, value_secs, decay_secs, incoming, gains))
    linear_rows = linear_out.reshape(CONTEXT_TOKENS, H * HD)
    key_blocks = soft_key.reshape(QBLOCKS, BLK, H, HD)
    value_blocks = soft_value.reshape(QBLOCKS, BLK, H, HD)
    query_blocks = soft_query.reshape(QBLOCKS, BLK, H, HD)
    rows_all = jnp.arange(QBLOCKS, dtype=jnp.int32)

    def one_block(pieces):
        query_blk, index_row, count_row, row_global = pieces
        keys_sel = jnp.take(key_blocks, index_row, axis=0)
        values_sel = jnp.take(value_blocks, index_row, axis=0)
        return attend(query_blk, keys_sel, values_sel, index_row, count_row, row_global)
    soft_out = lax.map(one_block, (query_blocks, block_index, block_count, rows_all))
    return (linear_rows, soft_out.reshape(CONTEXT_TOKENS, H * HD))
```

```python
import math

import jax
import jax.numpy as jnp
from jax import lax
from jax.sharding import PartitionSpec as P

BLK = 128
WIN_SEC = 2


EPS = 1e-06


def passed_along(block, axis, distance):
    devices = range(lax.axis_size(axis))
    route = [(i - distance, i) for i in devices if i - distance in devices]
    return lax.ppermute(block, axis, route)


def causal_mask(length):
    rows_iota = lax.broadcasted_iota(jnp.int32, (length, length), 0)
    cols_iota = lax.broadcasted_iota(jnp.int32, (length, length), 1)
    return cols_iota <= rows_iota


def to_blocks(matrix, heads):
    length, columns = matrix.shape
    return matrix.reshape(length // BLK, BLK, heads, columns // heads)


def block_state(carried, keys_blk, values_blk, cumul_blk, total_blk):
    factor = jnp.exp(total_blk[:, None] - cumul_blk).T
    decayed = (keys_blk.astype(jnp.float32) * factor[:, :, None]).astype(jnp.bfloat16)
    update = jnp.einsum("jhd,jhe->hde", decayed, values_blk, preferred_element_type=jnp.float32)
    return jnp.exp(total_blk)[:, None, None] * carried + update


def block_output(carried, query_blk, keys_blk, values_blk, cumul_blk):
    scores = jnp.einsum("thd,jhd->htj", query_blk, keys_blk, preferred_element_type=jnp.float32)
    differ = cumul_blk[:, :, None] - cumul_blk[:, None, :]
    allowed = causal_mask(query_blk.shape[0])
    weights = jnp.where(allowed[None], jnp.exp(jnp.minimum(differ, 0.0)), 0.0)
    mixing = (scores * weights).astype(jnp.bfloat16)
    inside = jnp.einsum("htj,jhd->thd", mixing, values_blk, preferred_element_type=jnp.float32)
    decayed_query = (query_blk.astype(jnp.float32) * jnp.exp(cumul_blk).T[:, :, None]).astype(
        jnp.bfloat16
    )
    across = jnp.einsum(
        "thd,hde->the",
        decayed_query,
        carried.astype(jnp.bfloat16),
        preferred_element_type=jnp.float32,
    )
    return inside + across


def combine_states(earlier, later):
    return (earlier[0] * later[0], later[0][:, None, None] * earlier[1] + later[1])


def carry_in(final, section_total):
    count, mine = (lax.axis_size("ctx"), lax.axis_index("ctx"))
    factor = jnp.exp(section_total)
    shifted = passed_along((factor, final), "ctx", 1)
    first = mine < 1
    running = (jnp.where(first, 1.0, shifted[0]), jnp.where(first, 0.0, shifted[1]))
    distance = 1
    while distance < count:
        earlier = passed_along(running, "ctx", distance)
        joined = combine_states(earlier, running)
        reached = mine >= distance
        running = jax.tree.map(lambda new, old: jnp.where(reached, new, old), joined, running)
        distance *= 2
    return running[1]


def linear_layer(linear_query, linear_key, linear_value, log_decay, norm_gain):
    length, columns = linear_query.shape
    heads = log_decay.shape[0]
    width = columns // heads
    blocks_here = length // BLK
    query_blocks = to_blocks(linear_query, heads)
    keys_blocks = to_blocks(linear_key, heads)
    values_blocks = to_blocks(linear_value, heads)
    per_block = log_decay.reshape(heads, blocks_here, BLK).transpose(1, 0, 2)
    cumulative = jnp.cumsum(per_block, axis=2)
    totals = cumulative[:, :, -1]
    section_cum = jnp.cumsum(log_decay, axis=1)
    section_total = section_cum[:, -1]
    carried = jnp.zeros((heads, width, width), jnp.float32)
    before = []
    for b in range(blocks_here):
        before.append(carried)
        carried = block_state(carried, keys_blocks[b], values_blocks[b], cumulative[b], totals[b])
    incoming = carry_in(carried, section_total)
    outputs = [
        block_output(before[b], query_blocks[b], keys_blocks[b], values_blocks[b], cumulative[b])
        for b in range(blocks_here)
    ]
    queries_flat = linear_query.reshape(length, heads, width)
    scaled = (queries_flat.astype(jnp.float32) * jnp.exp(section_cum).T[:, :, None]).astype(
        jnp.bfloat16
    )
    raw = jnp.concatenate(outputs, axis=0) + jnp.einsum(
        "thd,hde->the", scaled, incoming.astype(jnp.bfloat16), preferred_element_type=jnp.float32
    )
    square_mean = jnp.mean(raw * raw, axis=2, keepdims=True)
    normed = raw * lax.rsqrt(square_mean + EPS) * norm_gain.reshape(heads, width)
    return normed.astype(jnp.bfloat16).reshape(length, columns)


def attend(query_blk, keys_sel, values_sel, index_row, count_row, row_global):
    width = query_blk.shape[-1]
    inverse_root = 1.0 / math.sqrt(width)
    scores = (
        jnp.einsum("thd,kjhd->htkj", query_blk, keys_sel, preferred_element_type=jnp.float32)
        * inverse_root
    )
    slot_used = jnp.arange(index_row.shape[0], dtype=jnp.int32) < count_row
    off_diagonal = jnp.logical_not(index_row == row_global)
    allowed = slot_used[None, :, None] & (
        off_diagonal[None, :, None] | causal_mask(query_blk.shape[0])[:, None, :]
    )
    scores = jnp.where(allowed[None], scores, -jnp.inf)
    highest = jnp.max(scores, axis=(2, 3), keepdims=True)
    raised = jnp.exp(scores - highest)
    weights = (raised / jnp.sum(raised, axis=(2, 3), keepdims=True)).astype(jnp.bfloat16)
    output = jnp.einsum("htkj,kjhd->thd", weights, values_sel, preferred_element_type=jnp.float32)
    return output.astype(jnp.bfloat16)


def softmax_layer(soft_query, soft_key, soft_value, block_index, block_count, heads):
    length, columns = soft_query.shape
    per_section = length // BLK
    own_pair = (soft_key, soft_value)
    pieces = []
    for distance in range(WIN_SEC, 0, -1):
        pieces.append(passed_along((own_pair[0], own_pair[1]), "ctx", distance))
    window_key = jnp.concatenate([piece[0] for piece in pieces] + [soft_key], axis=0)
    window_value = jnp.concatenate([piece[1] for piece in pieces] + [soft_value], axis=0)
    key_blocks = to_blocks(window_key, heads)
    value_blocks = to_blocks(window_value, heads)
    section = lax.axis_index("ctx")
    first_block = (section - WIN_SEC) * per_section
    query_blocks = to_blocks(soft_query, heads)
    own_rows = section * per_section + jnp.arange(per_section, dtype=jnp.int32)

    def one_block(inputs):
        query_blk, index_row, count_row, row_global = inputs
        local_row = index_row - first_block
        keys_sel = jnp.take(key_blocks, local_row, axis=0)
        values_sel = jnp.take(value_blocks, local_row, axis=0)
        return attend(query_blk, keys_sel, values_sel, index_row, count_row, row_global)

    outputs = lax.map(one_block, (query_blocks, block_index, block_count, own_rows))
    return outputs.reshape(length, columns)


def local(
    linear_query,
    linear_key,
    linear_value,
    log_decay,
    norm_gain,
    soft_query,
    soft_key,
    soft_value,
    block_index,
    block_count,
):
    heads = log_decay.shape[0]
    linear_heads = linear_layer(linear_query, linear_key, linear_value, log_decay, norm_gain)
    softmax_heads = softmax_layer(soft_query, soft_key, soft_value, block_index, block_count, heads)
    result = (
        lax.all_to_all(linear_heads, "head", split_axis=0, concat_axis=1, tiled=True),
        lax.all_to_all(softmax_heads, "head", split_axis=0, concat_axis=1, tiled=True),
    )
    return (result[0], result[1])


def solution(mesh):
    in_specs = (
        P("ctx", "head"),
        P("ctx", "head"),
        P("ctx", "head"),
        P("head", "ctx"),
        P("head"),
        P("ctx", "head"),
        P("ctx", "head"),
        P("ctx", "head"),
        P("ctx", None),
        P("ctx"),
    )
    out_specs = (P(("ctx", "head"), None), P(("ctx", "head"), None))
    return jax.shard_map(local, mesh=mesh, in_specs=in_specs, out_specs=out_specs, check_vma=False)
```

```python
import math

import jax
import jax.numpy as jnp
from jax import lax
from jax.sharding import PartitionSpec as P

BLK = 128
WIN_SEC = 2


EPS = 1e-06


CTX = ("cy", "cz", "cc")


def passed_along(block, axis, distance, count):
    devices = range(count)
    route = [(i - distance, i) for i in devices if i - distance in devices]
    return lax.ppermute(block, axis, route)


def causal_mask(length):
    rows_iota = lax.broadcasted_iota(jnp.int32, (length, length), 0)
    cols_iota = lax.broadcasted_iota(jnp.int32, (length, length), 1)
    return cols_iota <= rows_iota


def to_blocks(matrix, heads):
    length, columns = matrix.shape
    return matrix.reshape(length // BLK, BLK, heads, columns // heads)


def block_state(carried, keys_blk, values_blk, cumul_blk, total_blk):
    factor = jnp.exp(total_blk[:, None] - cumul_blk).T
    decayed = (keys_blk.astype(jnp.float32) * factor[:, :, None]).astype(jnp.bfloat16)
    update = jnp.einsum("jhd,jhe->hde", decayed, values_blk, preferred_element_type=jnp.float32)
    return jnp.exp(total_blk)[:, None, None] * carried + update


def block_output(carried, query_blk, keys_blk, values_blk, cumul_blk):
    scores = jnp.einsum("thd,jhd->htj", query_blk, keys_blk, preferred_element_type=jnp.float32)
    differ = cumul_blk[:, :, None] - cumul_blk[:, None, :]
    allowed = causal_mask(query_blk.shape[0])
    weights = jnp.where(allowed[None], jnp.exp(jnp.minimum(differ, 0.0)), 0.0)
    mixing = (scores * weights).astype(jnp.bfloat16)
    inside = jnp.einsum("htj,jhd->thd", mixing, values_blk, preferred_element_type=jnp.float32)
    decayed_query = (query_blk.astype(jnp.float32) * jnp.exp(cumul_blk).T[:, :, None]).astype(
        jnp.bfloat16
    )
    across = jnp.einsum(
        "thd,hde->the",
        decayed_query,
        carried.astype(jnp.bfloat16),
        preferred_element_type=jnp.float32,
    )
    return inside + across


def packed(state, factor):
    heads, width, _ = state.shape
    return jnp.concatenate([state, jnp.broadcast_to(factor[:, None, None], (heads, 8, width))], axis=1)


def unpacked(both, width):
    return both[..., :width, :], both[..., width, 0]


def carry_in(final, section_total):
    heads, width, _ = final.shape
    half = heads // 2
    core, row, column = (lax.axis_index("cc"), lax.axis_index("cz"), lax.axis_index("cy"))
    pair_states, pair_factors = unpacked(
        lax.all_gather(packed(final, jnp.exp(section_total)), "cc"), width
    )
    low = core * half
    first = lax.dynamic_slice_in_dim(pair_states[0], low, half, 0)
    second = lax.dynamic_slice_in_dim(pair_states[1], low, half, 0)
    first_factor = lax.dynamic_slice_in_dim(pair_factors[0], low, half, 0)
    second_factor = lax.dynamic_slice_in_dim(pair_factors[1], low, half, 0)
    chip_state = second_factor[:, None, None] * first + second
    chip_factor = first_factor * second_factor
    row_states, row_factors = unpacked(
        lax.all_gather(packed(chip_state, chip_factor), "cz"), width
    )
    total = jnp.zeros_like(chip_state)
    total_factor = jnp.ones_like(chip_factor)
    before = total
    before_factor = total_factor
    for z in range(row_states.shape[0]):
        here = z == row
        before = jnp.where(here, total, before)
        before_factor = jnp.where(here, total_factor, before_factor)
        total = row_factors[z][:, None, None] * total + row_states[z]
        total_factor = total_factor * row_factors[z]
    column_states, column_factors = unpacked(
        lax.all_gather(packed(total, total_factor), "cy"), width
    )
    above = jnp.zeros_like(chip_state)
    for y in range(column_states.shape[0]):
        joined = column_factors[y][:, None, None] * above + column_states[y]
        above = jnp.where(y < column, joined, above)
    prefix_half = before_factor[:, None, None] * above + before
    prefix = lax.all_gather(prefix_half, "cc", axis=0, tiled=True)
    later = pair_factors[0][:, None, None] * prefix + pair_states[0]
    return jnp.where(core == 0, prefix, later)


def linear_layer(linear_query, linear_key, linear_value, log_decay, norm_gain):
    length, columns = linear_query.shape
    heads = log_decay.shape[0]
    width = columns // heads
    blocks_here = length // BLK
    query_blocks = to_blocks(linear_query, heads)
    keys_blocks = to_blocks(linear_key, heads)
    values_blocks = to_blocks(linear_value, heads)
    per_block = log_decay.reshape(heads, blocks_here, BLK).transpose(1, 0, 2)
    cumulative = jnp.cumsum(per_block, axis=2)
    totals = cumulative[:, :, -1]
    section_cum = jnp.cumsum(log_decay, axis=1)
    section_total = section_cum[:, -1]
    carried = jnp.zeros((heads, width, width), jnp.float32)
    before = []
    for b in range(blocks_here):
        before.append(carried)
        carried = block_state(carried, keys_blocks[b], values_blocks[b], cumulative[b], totals[b])
    incoming = carry_in(carried, section_total)
    outputs = [
        block_output(before[b], query_blocks[b], keys_blocks[b], values_blocks[b], cumulative[b])
        for b in range(blocks_here)
    ]
    queries_flat = linear_query.reshape(length, heads, width)
    scaled = (queries_flat.astype(jnp.float32) * jnp.exp(section_cum).T[:, :, None]).astype(
        jnp.bfloat16
    )
    raw = jnp.concatenate(outputs, axis=0) + jnp.einsum(
        "thd,hde->the", scaled, incoming.astype(jnp.bfloat16), preferred_element_type=jnp.float32
    )
    square_mean = jnp.mean(raw * raw, axis=2, keepdims=True)
    normed = raw * lax.rsqrt(square_mean + EPS) * norm_gain.reshape(heads, width)
    return normed.astype(jnp.bfloat16).reshape(length, columns)


def attend(query_blk, keys_sel, values_sel, index_row, count_row, row_global):
    width = query_blk.shape[-1]
    inverse_root = 1.0 / math.sqrt(width)
    scores = (
        jnp.einsum("thd,kjhd->htkj", query_blk, keys_sel, preferred_element_type=jnp.float32)
        * inverse_root
    )
    slot_used = jnp.arange(index_row.shape[0], dtype=jnp.int32) < count_row
    off_diagonal = jnp.logical_not(index_row == row_global)
    allowed = slot_used[None, :, None] & (
        off_diagonal[None, :, None] | causal_mask(query_blk.shape[0])[:, None, :]
    )
    scores = jnp.where(allowed[None], scores, -jnp.inf)
    highest = jnp.max(scores, axis=(2, 3), keepdims=True)
    raised = jnp.exp(scores - highest)
    weights = (raised / jnp.sum(raised, axis=(2, 3), keepdims=True)).astype(jnp.bfloat16)
    output = jnp.einsum("htkj,kjhd->thd", weights, values_sel, preferred_element_type=jnp.float32)
    return output.astype(jnp.bfloat16)


def softmax_layer(soft_query, soft_key, soft_value, block_index, block_count, heads, sections):
    length, columns = soft_query.shape
    per_section = length // BLK
    own_pair = (soft_key, soft_value)
    pieces = []
    for distance in range(WIN_SEC, 0, -1):
        pieces.append(passed_along((own_pair[0], own_pair[1]), CTX, distance, sections))
    window_key = jnp.concatenate([piece[0] for piece in pieces] + [soft_key], axis=0)
    window_value = jnp.concatenate([piece[1] for piece in pieces] + [soft_value], axis=0)
    key_blocks = to_blocks(window_key, heads)
    value_blocks = to_blocks(window_value, heads)
    section = lax.axis_index(CTX)
    first_block = (section - WIN_SEC) * per_section
    query_blocks = to_blocks(soft_query, heads)
    own_rows = section * per_section + jnp.arange(per_section, dtype=jnp.int32)

    def one_block(inputs):
        query_blk, index_row, count_row, row_global = inputs
        local_row = index_row - first_block
        keys_sel = jnp.take(key_blocks, local_row, axis=0)
        values_sel = jnp.take(value_blocks, local_row, axis=0)
        return attend(query_blk, keys_sel, values_sel, index_row, count_row, row_global)

    outputs = lax.map(one_block, (query_blocks, block_index, block_count, own_rows))
    return outputs.reshape(length, columns)


def local(
    linear_query,
    linear_key,
    linear_value,
    log_decay,
    norm_gain,
    soft_query,
    soft_key,
    soft_value,
    block_index,
    block_count,
):
    heads = log_decay.shape[0]
    linear_heads = linear_layer(linear_query, linear_key, linear_value, log_decay, norm_gain)
    sections = lax.psum(1, CTX)
    softmax_heads = softmax_layer(
        soft_query, soft_key, soft_value, block_index, block_count, heads, sections
    )
    result = (
        lax.all_to_all(linear_heads, "head", split_axis=0, concat_axis=1, tiled=True),
        lax.all_to_all(softmax_heads, "head", split_axis=0, concat_axis=1, tiled=True),
    )
    return (result[0], result[1])


def solution(mesh):
    ctx, head = mesh.devices.shape
    split = mesh.devices.reshape(ctx // 16, 8, 2, head)
    mesh = jax.sharding.Mesh(split, CTX + ("head",))
    rows = P(CTX, "head")
    in_specs = (
        rows,
        rows,
        rows,
        P("head", CTX),
        P("head"),
        rows,
        rows,
        rows,
        P(CTX, None),
        P(CTX),
    )
    out_specs = (P(CTX + ("head",), None), P(CTX + ("head",), None))
    return jax.shard_map(local, mesh=mesh, in_specs=in_specs, out_specs=out_specs, check_vma=False)
```

```python
import math

import jax
import jax.numpy as jnp
from jax import lax
from jax.sharding import PartitionSpec as P

BLK = 128
WIN_SEC = 2


EPS = 1e-06


CTX = ("cy", "cz", "cc")


def passed_along(block, axis, distance, count):
    devices = range(count)
    route = [(i - distance, i) for i in devices if i - distance in devices]
    return lax.ppermute(block, axis, route)


def causal_mask(length):
    rows_iota = lax.broadcasted_iota(jnp.int32, (length, length), 0)
    cols_iota = lax.broadcasted_iota(jnp.int32, (length, length), 1)
    return cols_iota <= rows_iota


def to_blocks(matrix, heads):
    length, columns = matrix.shape
    return matrix.reshape(length // BLK, BLK, heads, columns // heads)


def block_state(carried, keys_blk, values_blk, cumul_blk, total_blk):
    factor = jnp.exp(total_blk[:, None] - cumul_blk).T
    decayed = (keys_blk.astype(jnp.float32) * factor[:, :, None]).astype(jnp.bfloat16)
    update = jnp.einsum("jhd,jhe->hde", decayed, values_blk, preferred_element_type=jnp.float32)
    return jnp.exp(total_blk)[:, None, None] * carried + update


def block_output(carried, query_blk, keys_blk, values_blk, cumul_blk):
    scores = jnp.einsum("thd,jhd->htj", query_blk, keys_blk, preferred_element_type=jnp.float32)
    differ = cumul_blk[:, :, None] - cumul_blk[:, None, :]
    allowed = causal_mask(query_blk.shape[0])
    weights = jnp.where(allowed[None], jnp.exp(jnp.minimum(differ, 0.0)), 0.0)
    mixing = (scores * weights).astype(jnp.bfloat16)
    inside = jnp.einsum("htj,jhd->thd", mixing, values_blk, preferred_element_type=jnp.float32)
    decayed_query = (query_blk.astype(jnp.float32) * jnp.exp(cumul_blk).T[:, :, None]).astype(
        jnp.bfloat16
    )
    across = jnp.einsum(
        "thd,hde->the",
        decayed_query,
        carried.astype(jnp.bfloat16),
        preferred_element_type=jnp.float32,
    )
    return inside + across


def packed(state, factor):
    heads, width, _ = state.shape
    return jnp.concatenate([state, jnp.broadcast_to(factor[:, None, None], (heads, 8, width))], axis=1)


def unpacked(both, width):
    return both[..., :width, :], both[..., width, 0]


def swapped(block):
    return lax.ppermute(block, "cc", [(0, 1), (1, 0)])


def carry_in(final, section_total):
    heads, width, _ = final.shape
    half = heads // 2
    core, row, column = (lax.axis_index("cc"), lax.axis_index("cz"), lax.axis_index("cy"))
    factor = jnp.exp(section_total)
    other_state, other_factor = unpacked(swapped(packed(final, factor)), width)
    on_first = core == 0
    first_state = jnp.where(on_first, final, other_state)
    first_all = jnp.where(on_first, factor, other_factor)
    second_state = jnp.where(on_first, other_state, final)
    second_all = jnp.where(on_first, other_factor, factor)
    low = core * half
    first = lax.dynamic_slice_in_dim(first_state, low, half, 0)
    second = lax.dynamic_slice_in_dim(second_state, low, half, 0)
    first_factor = lax.dynamic_slice_in_dim(first_all, low, half, 0)
    second_factor = lax.dynamic_slice_in_dim(second_all, low, half, 0)
    chip_state = second_factor[:, None, None] * first + second
    chip_factor = first_factor * second_factor
    row_states, row_factors = unpacked(
        lax.all_gather(packed(chip_state, chip_factor), "cz"), width
    )
    total = jnp.zeros_like(chip_state)
    total_factor = jnp.ones_like(chip_factor)
    before = total
    before_factor = total_factor
    for z in range(row_states.shape[0]):
        here = z == row
        before = jnp.where(here, total, before)
        before_factor = jnp.where(here, total_factor, before_factor)
        total = row_factors[z][:, None, None] * total + row_states[z]
        total_factor = total_factor * row_factors[z]
    column_states, column_factors = unpacked(
        lax.all_gather(packed(total, total_factor), "cy"), width
    )
    above = jnp.zeros_like(chip_state)
    for y in range(column_states.shape[0]):
        joined = column_factors[y][:, None, None] * above + column_states[y]
        above = jnp.where(y < column, joined, above)
    prefix_half = before_factor[:, None, None] * above + before
    other_half = swapped(prefix_half)
    prefix = jnp.where(
        on_first,
        jnp.concatenate([prefix_half, other_half], axis=0),
        jnp.concatenate([other_half, prefix_half], axis=0),
    )
    later = first_all[:, None, None] * prefix + first_state
    return jnp.where(on_first, prefix, later)


def linear_layer(linear_query, linear_key, linear_value, log_decay, norm_gain):
    length, columns = linear_query.shape
    heads = log_decay.shape[0]
    width = columns // heads
    blocks_here = length // BLK
    query_blocks = to_blocks(linear_query, heads)
    keys_blocks = to_blocks(linear_key, heads)
    values_blocks = to_blocks(linear_value, heads)
    per_block = log_decay.reshape(heads, blocks_here, BLK).transpose(1, 0, 2)
    cumulative = jnp.cumsum(per_block, axis=2)
    totals = cumulative[:, :, -1]
    section_cum = jnp.cumsum(log_decay, axis=1)
    section_total = section_cum[:, -1]
    carried = jnp.zeros((heads, width, width), jnp.float32)
    before = []
    for b in range(blocks_here):
        before.append(carried)
        carried = block_state(carried, keys_blocks[b], values_blocks[b], cumulative[b], totals[b])
    incoming = carry_in(carried, section_total)
    outputs = [
        block_output(before[b], query_blocks[b], keys_blocks[b], values_blocks[b], cumulative[b])
        for b in range(blocks_here)
    ]
    queries_flat = linear_query.reshape(length, heads, width)
    scaled = (queries_flat.astype(jnp.float32) * jnp.exp(section_cum).T[:, :, None]).astype(
        jnp.bfloat16
    )
    raw = jnp.concatenate(outputs, axis=0) + jnp.einsum(
        "thd,hde->the", scaled, incoming.astype(jnp.bfloat16), preferred_element_type=jnp.float32
    )
    square_mean = jnp.mean(raw * raw, axis=2, keepdims=True)
    normed = raw * lax.rsqrt(square_mean + EPS) * norm_gain.reshape(heads, width)
    return normed.astype(jnp.bfloat16).reshape(length, columns)


def attend(query_blk, keys_sel, values_sel, allowed):
    width = query_blk.shape[-1]
    inverse_root = 1.0 / math.sqrt(width)
    scores = (
        jnp.einsum("thd,kjhd->htkj", query_blk, keys_sel, preferred_element_type=jnp.float32)
        * inverse_root
    )
    scores = jnp.where(allowed[None], scores, -jnp.inf)
    highest = jnp.max(scores, axis=(2, 3), keepdims=True)
    raised = jnp.exp(scores - highest)
    weights = (raised / jnp.sum(raised, axis=(2, 3), keepdims=True)).astype(jnp.bfloat16)
    output = jnp.einsum("htkj,kjhd->thd", weights, values_sel, preferred_element_type=jnp.float32)
    return output.astype(jnp.bfloat16)


def softmax_layer(soft_query, soft_key, soft_value, block_index, block_count, heads, sections):
    length, columns = soft_query.shape
    per_section = length // BLK
    slots = block_index.shape[1]
    own_pair = (soft_key, soft_value)
    pieces = []
    for distance in range(WIN_SEC, 0, -1):
        pieces.append(passed_along((own_pair[0], own_pair[1]), CTX, distance, sections))
    window_key = jnp.concatenate([piece[0] for piece in pieces] + [soft_key], axis=0)
    window_value = jnp.concatenate([piece[1] for piece in pieces] + [soft_value], axis=0)
    key_blocks = to_blocks(window_key, heads)
    value_blocks = to_blocks(window_value, heads)
    section = lax.axis_index(CTX)
    first_block = (section - WIN_SEC) * per_section
    query_blocks = to_blocks(soft_query, heads)
    causal = causal_mask(BLK)
    slot_ids = jnp.arange(slots, dtype=jnp.int32)
    outputs = []
    for b in range(per_section):
        row_global = section * per_section + b
        low = b + WIN_SEC * per_section - (slots - 1)
        candidates = first_block + low + jnp.arange(slots, dtype=jnp.int32)
        used = slot_ids < block_count[b]
        matches = (block_index[b][None, :] == candidates[:, None]) & used[None, :]
        named = jnp.any(matches, axis=1)
        off_diagonal = candidates != row_global
        allowed = named[None, :, None] & (off_diagonal[None, :, None] | causal[:, None, :])
        outputs.append(
            attend(
                query_blocks[b],
                key_blocks[low : low + slots],
                value_blocks[low : low + slots],
                allowed,
            )
        )
    return jnp.concatenate(outputs, axis=0).reshape(length, columns)


def local(
    linear_query,
    linear_key,
    linear_value,
    log_decay,
    norm_gain,
    soft_query,
    soft_key,
    soft_value,
    block_index,
    block_count,
):
    heads = log_decay.shape[0]
    linear_heads = linear_layer(linear_query, linear_key, linear_value, log_decay, norm_gain)
    sections = lax.psum(1, CTX)
    softmax_heads = softmax_layer(
        soft_query, soft_key, soft_value, block_index, block_count, heads, sections
    )
    result = (
        lax.all_to_all(linear_heads, "head", split_axis=0, concat_axis=1, tiled=True),
        lax.all_to_all(softmax_heads, "head", split_axis=0, concat_axis=1, tiled=True),
    )
    return (result[0], result[1])


def solution(mesh):
    ctx, head = mesh.devices.shape
    split = mesh.devices.reshape(ctx // 16, 8, 2, head)
    mesh = jax.sharding.Mesh(split, CTX + ("head",))
    rows = P(CTX, "head")
    in_specs = (
        rows,
        rows,
        rows,
        P("head", CTX),
        P("head"),
        rows,
        rows,
        rows,
        P(CTX, None),
        P(CTX),
    )
    out_specs = (P(CTX + ("head",), None), P(CTX + ("head",), None))
    return jax.shard_map(local, mesh=mesh, in_specs=in_specs, out_specs=out_specs, check_vma=False)
```

```python
import math

import jax
import jax.numpy as jnp
from jax import lax
from jax.sharding import PartitionSpec as P

BLK = 128
WIN_SEC = 2


EPS = 1e-06


CTX = ("cy", "cz", "cc")


def passed_along(block, axis, distance, count):
    devices = range(count)
    route = [(i - distance, i) for i in devices if i - distance in devices]
    return lax.ppermute(block, axis, route)


def causal_mask(length):
    rows_iota = lax.broadcasted_iota(jnp.int32, (length, length), 0)
    cols_iota = lax.broadcasted_iota(jnp.int32, (length, length), 1)
    return cols_iota <= rows_iota


def to_blocks(matrix, heads):
    length, columns = matrix.shape
    return matrix.reshape(length // BLK, BLK, heads, columns // heads)


def block_state(carried, keys_blk, values_blk, cumul_blk, total_blk):
    factor = jnp.exp(total_blk[:, None] - cumul_blk).T
    decayed = (keys_blk.astype(jnp.float32) * factor[:, :, None]).astype(jnp.bfloat16)
    update = jnp.einsum("jhd,jhe->hde", decayed, values_blk, preferred_element_type=jnp.float32)
    return jnp.exp(total_blk)[:, None, None] * carried + update


def block_output(carried, query_blk, keys_blk, values_blk, cumul_blk):
    scores = jnp.einsum("thd,jhd->htj", query_blk, keys_blk, preferred_element_type=jnp.float32)
    differ = cumul_blk[:, :, None] - cumul_blk[:, None, :]
    allowed = causal_mask(query_blk.shape[0])
    weights = jnp.where(allowed[None], jnp.exp(jnp.minimum(differ, 0.0)), 0.0)
    mixing = (scores * weights).astype(jnp.bfloat16)
    inside = jnp.einsum("htj,jhd->thd", mixing, values_blk, preferred_element_type=jnp.float32)
    decayed_query = (query_blk.astype(jnp.float32) * jnp.exp(cumul_blk).T[:, :, None]).astype(
        jnp.bfloat16
    )
    across = jnp.einsum(
        "thd,hde->the",
        decayed_query,
        carried.astype(jnp.bfloat16),
        preferred_element_type=jnp.float32,
    )
    return inside + across


def packed(state, factor):
    heads, width, _ = state.shape
    return jnp.concatenate([state, jnp.broadcast_to(factor[:, None, None], (heads, 8, width))], axis=1)


def unpacked(both, width):
    return both[..., :width, :], both[..., width, 0]


def swapped(block):
    return lax.ppermute(block, "cc", [(0, 1), (1, 0)])


def carry_in(final, section_total):
    heads, width, _ = final.shape
    half = heads // 2
    core, row, column = (lax.axis_index("cc"), lax.axis_index("cz"), lax.axis_index("cy"))
    factor = jnp.exp(section_total)
    other_state, other_factor = unpacked(swapped(packed(final, factor)), width)
    on_first = core == 0
    first_state = jnp.where(on_first, final, other_state)
    first_all = jnp.where(on_first, factor, other_factor)
    second_state = jnp.where(on_first, other_state, final)
    second_all = jnp.where(on_first, other_factor, factor)
    low = core * half
    first = lax.dynamic_slice_in_dim(first_state, low, half, 0)
    second = lax.dynamic_slice_in_dim(second_state, low, half, 0)
    first_factor = lax.dynamic_slice_in_dim(first_all, low, half, 0)
    second_factor = lax.dynamic_slice_in_dim(second_all, low, half, 0)
    chip_state = second_factor[:, None, None] * first + second
    chip_factor = first_factor * second_factor
    row_states, row_factors = unpacked(
        lax.all_gather(packed(chip_state, chip_factor), "cz"), width
    )
    total = jnp.zeros_like(chip_state)
    total_factor = jnp.ones_like(chip_factor)
    before = total
    before_factor = total_factor
    for z in range(row_states.shape[0]):
        here = z == row
        before = jnp.where(here, total, before)
        before_factor = jnp.where(here, total_factor, before_factor)
        total = row_factors[z][:, None, None] * total + row_states[z]
        total_factor = total_factor * row_factors[z]
    column_states, column_factors = unpacked(
        lax.all_gather(packed(total, total_factor), "cy"), width
    )
    above = jnp.zeros_like(chip_state)
    for y in range(column_states.shape[0]):
        joined = column_factors[y][:, None, None] * above + column_states[y]
        above = jnp.where(y < column, joined, above)
    prefix_half = before_factor[:, None, None] * above + before
    other_half = swapped(prefix_half)
    prefix = jnp.where(
        on_first,
        jnp.concatenate([prefix_half, other_half], axis=0),
        jnp.concatenate([other_half, prefix_half], axis=0),
    )
    later = first_all[:, None, None] * prefix + first_state
    return jnp.where(on_first, prefix, later)


def linear_layer(linear_query, linear_key, linear_value, log_decay, norm_gain):
    length, columns = linear_query.shape
    heads = log_decay.shape[0]
    width = columns // heads
    blocks_here = length // BLK
    query_blocks = to_blocks(linear_query, heads)
    keys_blocks = to_blocks(linear_key, heads)
    values_blocks = to_blocks(linear_value, heads)
    per_block = log_decay.reshape(heads, blocks_here, BLK).transpose(1, 0, 2)
    cumulative = jnp.cumsum(per_block, axis=2)
    totals = cumulative[:, :, -1]
    section_cum = jnp.cumsum(log_decay, axis=1)
    section_total = section_cum[:, -1]
    carried = jnp.zeros((heads, width, width), jnp.float32)
    before = []
    for b in range(blocks_here):
        before.append(carried)
        carried = block_state(carried, keys_blocks[b], values_blocks[b], cumulative[b], totals[b])
    incoming = carry_in(carried, section_total)
    outputs = [
        block_output(before[b], query_blocks[b], keys_blocks[b], values_blocks[b], cumulative[b])
        for b in range(blocks_here)
    ]
    queries_flat = linear_query.reshape(length, heads, width)
    scaled = (queries_flat.astype(jnp.float32) * jnp.exp(section_cum).T[:, :, None]).astype(
        jnp.bfloat16
    )
    raw = jnp.concatenate(outputs, axis=0) + jnp.einsum(
        "thd,hde->the", scaled, incoming.astype(jnp.bfloat16), preferred_element_type=jnp.float32
    )
    square_mean = jnp.mean(raw * raw, axis=2, keepdims=True)
    normed = raw * lax.rsqrt(square_mean + EPS) * norm_gain.reshape(heads, width)
    return normed.astype(jnp.bfloat16).reshape(length, columns)


def attend(query_blk, keys_sel, values_sel, allowed):
    width = query_blk.shape[-1]
    inverse_root = 1.0 / math.sqrt(width)
    scores = (
        jnp.einsum("thd,kjhd->htkj", query_blk, keys_sel, preferred_element_type=jnp.float32)
        * inverse_root
    )
    scores = jnp.where(allowed[None], scores, -jnp.inf)
    highest = jnp.max(scores, axis=(2, 3), keepdims=True)
    raised = jnp.exp(scores - highest)
    weights = (raised / jnp.sum(raised, axis=(2, 3), keepdims=True)).astype(jnp.bfloat16)
    output = jnp.einsum("htkj,kjhd->thd", weights, values_sel, preferred_element_type=jnp.float32)
    return output.astype(jnp.bfloat16)


def softmax_layer(soft_query, soft_key, soft_value, block_index, block_count, heads, sections):
    length, columns = soft_query.shape
    per_section = length // BLK
    slots = block_index.shape[1]
    own_pair = (soft_key, soft_value)
    farther = passed_along(own_pair, CTX, 2, sections)
    on_first = lax.axis_index("cc") == 0
    handed = jax.tree.map(lambda own, far: jnp.where(on_first, own, far), own_pair, farther)
    nearer = swapped(handed)
    pieces = [farther, nearer]
    window_key = jnp.concatenate([piece[0] for piece in pieces] + [soft_key], axis=0)
    window_value = jnp.concatenate([piece[1] for piece in pieces] + [soft_value], axis=0)
    key_blocks = to_blocks(window_key, heads)
    value_blocks = to_blocks(window_value, heads)
    section = lax.axis_index(CTX)
    first_block = (section - WIN_SEC) * per_section
    query_blocks = to_blocks(soft_query, heads)
    causal = causal_mask(BLK)
    slot_ids = jnp.arange(slots, dtype=jnp.int32)
    outputs = []
    for b in range(per_section):
        row_global = section * per_section + b
        low = b + WIN_SEC * per_section - (slots - 1)
        candidates = first_block + low + jnp.arange(slots, dtype=jnp.int32)
        used = slot_ids < block_count[b]
        matches = (block_index[b][None, :] == candidates[:, None]) & used[None, :]
        named = jnp.any(matches, axis=1)
        off_diagonal = candidates != row_global
        allowed = named[None, :, None] & (off_diagonal[None, :, None] | causal[:, None, :])
        outputs.append(
            attend(
                query_blocks[b],
                key_blocks[low : low + slots],
                value_blocks[low : low + slots],
                allowed,
            )
        )
    return jnp.concatenate(outputs, axis=0).reshape(length, columns)


def local(
    linear_query,
    linear_key,
    linear_value,
    log_decay,
    norm_gain,
    soft_query,
    soft_key,
    soft_value,
    block_index,
    block_count,
):
    heads = log_decay.shape[0]
    linear_heads = linear_layer(linear_query, linear_key, linear_value, log_decay, norm_gain)
    sections = lax.psum(1, CTX)
    softmax_heads = softmax_layer(
        soft_query, soft_key, soft_value, block_index, block_count, heads, sections
    )
    result = (
        lax.all_to_all(linear_heads, "head", split_axis=0, concat_axis=1, tiled=True),
        lax.all_to_all(softmax_heads, "head", split_axis=0, concat_axis=1, tiled=True),
    )
    return (result[0], result[1])


def solution(mesh):
    ctx, head = mesh.devices.shape
    split = mesh.devices.reshape(ctx // 16, 8, 2, head)
    mesh = jax.sharding.Mesh(split, CTX + ("head",))
    rows = P(CTX, "head")
    in_specs = (
        rows,
        rows,
        rows,
        P("head", CTX),
        P("head"),
        rows,
        rows,
        rows,
        P(CTX, None),
        P(CTX),
    )
    out_specs = (P(CTX + ("head",), None), P(CTX + ("head",), None))
    return jax.shard_map(local, mesh=mesh, in_specs=in_specs, out_specs=out_specs, check_vma=False)
```

```python
import math

import jax
import jax.numpy as jnp
from jax import lax
from jax.sharding import PartitionSpec as P

BLK = 128
WIN_SEC = 2


EPS = 1e-06


CTX = ("cy", "cz", "cc")


def passed_along(block, axis, distance, count):
    devices = range(count)
    route = [(i - distance, i) for i in devices if i - distance in devices]
    return lax.ppermute(block, axis, route)


def causal_mask(length):
    rows_iota = lax.broadcasted_iota(jnp.int32, (length, length), 0)
    cols_iota = lax.broadcasted_iota(jnp.int32, (length, length), 1)
    return cols_iota <= rows_iota


def to_blocks(matrix, heads):
    length, columns = matrix.shape
    return matrix.reshape(length // BLK, BLK, heads, columns // heads)


def block_state(carried, keys_blk, values_blk, cumul_blk, total_blk):
    factor = jnp.exp(total_blk[:, None] - cumul_blk).T
    decayed = (keys_blk.astype(jnp.float32) * factor[:, :, None]).astype(jnp.bfloat16)
    update = jnp.einsum("jhd,jhe->hde", decayed, values_blk, preferred_element_type=jnp.float32)
    return jnp.exp(total_blk)[:, None, None] * carried + update


def block_output(carried, query_blk, keys_blk, values_blk, cumul_blk):
    scores = jnp.einsum("thd,jhd->htj", query_blk, keys_blk, preferred_element_type=jnp.float32)
    differ = cumul_blk[:, :, None] - cumul_blk[:, None, :]
    allowed = causal_mask(query_blk.shape[0])
    weights = jnp.where(allowed[None], jnp.exp(jnp.minimum(differ, 0.0)), 0.0)
    mixing = (scores * weights).astype(jnp.bfloat16)
    inside = jnp.einsum("htj,jhd->thd", mixing, values_blk, preferred_element_type=jnp.float32)
    decayed_query = (query_blk.astype(jnp.float32) * jnp.exp(cumul_blk).T[:, :, None]).astype(
        jnp.bfloat16
    )
    across = jnp.einsum(
        "thd,hde->the",
        decayed_query,
        carried.astype(jnp.bfloat16),
        preferred_element_type=jnp.float32,
    )
    return inside + across


def packed(state, factor):
    heads, width, _ = state.shape
    return jnp.concatenate([state, jnp.broadcast_to(factor[:, None, None], (heads, 8, width))], axis=1)


def unpacked(both, width):
    return both[..., :width, :], both[..., width, 0]


def swapped(block):
    return lax.ppermute(block, "cc", [(0, 1), (1, 0)])


def carry_in(final, section_total, held):
    heads, width, _ = final.shape
    half = heads // 2
    core, row, column = (lax.axis_index("cc"), lax.axis_index("cz"), lax.axis_index("cy"))
    factor = jnp.exp(section_total)
    other_state, other_factor = unpacked(swapped(packed(final, factor)), width)
    on_first = core == 0
    first_state = jnp.where(on_first, final, other_state)
    first_all = jnp.where(on_first, factor, other_factor)
    second_state = jnp.where(on_first, other_state, final)
    second_all = jnp.where(on_first, other_factor, factor)
    low = core * half
    first = lax.dynamic_slice_in_dim(first_state, low, half, 0)
    second = lax.dynamic_slice_in_dim(second_state, low, half, 0)
    first_factor = lax.dynamic_slice_in_dim(first_all, low, half, 0)
    second_factor = lax.dynamic_slice_in_dim(second_all, low, half, 0)
    chip_state = second_factor[:, None, None] * first + second
    chip_factor = first_factor * second_factor
    row_states, row_factors = unpacked(
        lax.all_gather(packed(chip_state, chip_factor), "cz"), width
    )
    total = jnp.zeros_like(chip_state)
    total_factor = jnp.ones_like(chip_factor)
    before = total
    before_factor = total_factor
    for z in range(row_states.shape[0]):
        here = z == row
        before = jnp.where(here, total, before)
        before_factor = jnp.where(here, total_factor, before_factor)
        total = row_factors[z][:, None, None] * total + row_states[z]
        total_factor = total_factor * row_factors[z]
    column_packed = lax.all_gather(packed(total, total_factor), "cy")
    column_packed, held = lax.optimization_barrier((column_packed, held))
    column_states, column_factors = unpacked(column_packed, width)
    above = jnp.zeros_like(chip_state)
    for y in range(column_states.shape[0]):
        joined = column_factors[y][:, None, None] * above + column_states[y]
        above = jnp.where(y < column, joined, above)
    prefix_half = before_factor[:, None, None] * above + before
    other_half = swapped(prefix_half)
    prefix = jnp.where(
        on_first,
        jnp.concatenate([prefix_half, other_half], axis=0),
        jnp.concatenate([other_half, prefix_half], axis=0),
    )
    later = first_all[:, None, None] * prefix + first_state
    return jnp.where(on_first, prefix, later), held


def linear_layer(linear_query, linear_key, linear_value, log_decay, norm_gain, held):
    length, columns = linear_query.shape
    heads = log_decay.shape[0]
    width = columns // heads
    blocks_here = length // BLK
    query_blocks = to_blocks(linear_query, heads)
    keys_blocks = to_blocks(linear_key, heads)
    values_blocks = to_blocks(linear_value, heads)
    per_block = log_decay.reshape(heads, blocks_here, BLK).transpose(1, 0, 2)
    cumulative = jnp.cumsum(per_block, axis=2)
    totals = cumulative[:, :, -1]
    section_cum = jnp.cumsum(log_decay, axis=1)
    section_total = section_cum[:, -1]
    carried = jnp.zeros((heads, width, width), jnp.float32)
    before = []
    for b in range(blocks_here):
        before.append(carried)
        carried = block_state(carried, keys_blocks[b], values_blocks[b], cumulative[b], totals[b])
    incoming, held = carry_in(carried, section_total, held)
    outputs = [
        block_output(before[b], query_blocks[b], keys_blocks[b], values_blocks[b], cumulative[b])
        for b in range(blocks_here)
    ]
    queries_flat = linear_query.reshape(length, heads, width)
    scaled = (queries_flat.astype(jnp.float32) * jnp.exp(section_cum).T[:, :, None]).astype(
        jnp.bfloat16
    )
    raw = jnp.concatenate(outputs, axis=0) + jnp.einsum(
        "thd,hde->the", scaled, incoming.astype(jnp.bfloat16), preferred_element_type=jnp.float32
    )
    square_mean = jnp.mean(raw * raw, axis=2, keepdims=True)
    normed = raw * lax.rsqrt(square_mean + EPS) * norm_gain.reshape(heads, width)
    return normed.astype(jnp.bfloat16).reshape(length, columns), held


def attend(query_blk, keys_sel, values_sel, allowed):
    width = query_blk.shape[-1]
    inverse_root = 1.0 / math.sqrt(width)
    scores = (
        jnp.einsum("thd,kjhd->htkj", query_blk, keys_sel, preferred_element_type=jnp.float32)
        * inverse_root
    )
    scores = jnp.where(allowed[None], scores, -jnp.inf)
    highest = jnp.max(scores, axis=(2, 3), keepdims=True)
    raised = jnp.exp(scores - highest)
    weights = (raised / jnp.sum(raised, axis=(2, 3), keepdims=True)).astype(jnp.bfloat16)
    output = jnp.einsum("htkj,kjhd->thd", weights, values_sel, preferred_element_type=jnp.float32)
    return output.astype(jnp.bfloat16)


def softmax_layer(soft_query, soft_key, soft_value, block_index, block_count, heads, sections):
    length, columns = soft_query.shape
    per_section = length // BLK
    slots = block_index.shape[1]
    own_pair = (soft_key, soft_value)
    farther = passed_along(own_pair, CTX, 2, sections)
    on_first = lax.axis_index("cc") == 0
    handed = jax.tree.map(lambda own, far: jnp.where(on_first, own, far), own_pair, farther)
    nearer = swapped(handed)
    pieces = [farther, nearer]
    window_key = jnp.concatenate([piece[0] for piece in pieces] + [soft_key], axis=0)
    window_value = jnp.concatenate([piece[1] for piece in pieces] + [soft_value], axis=0)
    key_blocks = to_blocks(window_key, heads)
    value_blocks = to_blocks(window_value, heads)
    section = lax.axis_index(CTX)
    first_block = (section - WIN_SEC) * per_section
    query_blocks = to_blocks(soft_query, heads)
    causal = causal_mask(BLK)
    slot_ids = jnp.arange(slots, dtype=jnp.int32)
    outputs = []
    for b in range(per_section):
        row_global = section * per_section + b
        low = b + WIN_SEC * per_section - (slots - 1)
        candidates = first_block + low + jnp.arange(slots, dtype=jnp.int32)
        used = slot_ids < block_count[b]
        matches = (block_index[b][None, :] == candidates[:, None]) & used[None, :]
        named = jnp.any(matches, axis=1)
        off_diagonal = candidates != row_global
        allowed = named[None, :, None] & (off_diagonal[None, :, None] | causal[:, None, :])
        outputs.append(
            attend(
                query_blocks[b],
                key_blocks[low : low + slots],
                value_blocks[low : low + slots],
                allowed,
            )
        )
    return jnp.concatenate(outputs, axis=0).reshape(length, columns)


def local(
    linear_query,
    linear_key,
    linear_value,
    log_decay,
    norm_gain,
    soft_query,
    soft_key,
    soft_value,
    block_index,
    block_count,
):
    heads = log_decay.shape[0]
    linear_heads, (soft_key, soft_value) = linear_layer(
        linear_query, linear_key, linear_value, log_decay, norm_gain, (soft_key, soft_value)
    )
    sections = lax.psum(1, CTX)
    softmax_heads = softmax_layer(
        soft_query, soft_key, soft_value, block_index, block_count, heads, sections
    )
    result = (
        lax.all_to_all(linear_heads, "head", split_axis=0, concat_axis=1, tiled=True),
        lax.all_to_all(softmax_heads, "head", split_axis=0, concat_axis=1, tiled=True),
    )
    return (result[0], result[1])


def solution(mesh):
    ctx, head = mesh.devices.shape
    split = mesh.devices.reshape(ctx // 16, 8, 2, head)
    mesh = jax.sharding.Mesh(split, CTX + ("head",))
    rows = P(CTX, "head")
    in_specs = (
        rows,
        rows,
        rows,
        P("head", CTX),
        P("head"),
        rows,
        rows,
        rows,
        P(CTX, None),
        P(CTX),
    )
    out_specs = (P(CTX + ("head",), None), P(CTX + ("head",), None))
    return jax.shard_map(local, mesh=mesh, in_specs=in_specs, out_specs=out_specs, check_vma=False)
```

```python
import math

import jax
import jax.numpy as jnp
from jax import lax
from jax.sharding import PartitionSpec as P

BLK = 128
WIN_SEC = 2


EPS = 1e-06


CTX = ("cy", "cz", "cc")


def passed_along(block, axis, distance, count):
    devices = range(count)
    route = [(i - distance, i) for i in devices if i - distance in devices]
    return lax.ppermute(block, axis, route)


def causal_mask(length):
    rows_iota = lax.broadcasted_iota(jnp.int32, (length, length), 0)
    cols_iota = lax.broadcasted_iota(jnp.int32, (length, length), 1)
    return cols_iota <= rows_iota


def to_blocks(matrix, heads):
    length, columns = matrix.shape
    return matrix.reshape(length // BLK, BLK, heads, columns // heads)


def block_state(carried, keys_blk, values_blk, cumul_blk, total_blk):
    factor = jnp.exp(total_blk[:, None] - cumul_blk).T
    decayed = (keys_blk.astype(jnp.float32) * factor[:, :, None]).astype(jnp.bfloat16)
    update = jnp.einsum("jhd,jhe->hde", decayed, values_blk, preferred_element_type=jnp.float32)
    return jnp.exp(total_blk)[:, None, None] * carried + update


def block_output(carried, query_blk, keys_blk, values_blk, cumul_blk):
    scores = jnp.einsum("thd,jhd->htj", query_blk, keys_blk, preferred_element_type=jnp.float32)
    differ = cumul_blk[:, :, None] - cumul_blk[:, None, :]
    allowed = causal_mask(query_blk.shape[0])
    weights = jnp.where(allowed[None], jnp.exp(jnp.minimum(differ, 0.0)), 0.0)
    mixing = (scores * weights).astype(jnp.bfloat16)
    inside = jnp.einsum("htj,jhd->thd", mixing, values_blk, preferred_element_type=jnp.float32)
    decayed_query = (query_blk.astype(jnp.float32) * jnp.exp(cumul_blk).T[:, :, None]).astype(
        jnp.bfloat16
    )
    across = jnp.einsum(
        "thd,hde->the",
        decayed_query,
        carried.astype(jnp.bfloat16),
        preferred_element_type=jnp.float32,
    )
    return inside + across


def packed(state, factor):
    heads, width, _ = state.shape
    return jnp.concatenate([state, jnp.broadcast_to(factor[:, None, None], (heads, 8, width))], axis=1)


def unpacked(both, width):
    return both[..., :width, :], both[..., width, 0]


def swapped(block):
    return lax.ppermute(block, "cc", [(0, 1), (1, 0)])


def carry_in(final, section_total, held):
    heads, width, _ = final.shape
    half = heads // 2
    core, row, column = (lax.axis_index("cc"), lax.axis_index("cz"), lax.axis_index("cy"))
    factor = jnp.exp(section_total)
    other_state, other_factor = unpacked(swapped(packed(final, factor)), width)
    on_first = core == 0
    first_state = jnp.where(on_first, final, other_state)
    first_all = jnp.where(on_first, factor, other_factor)
    second_state = jnp.where(on_first, other_state, final)
    second_all = jnp.where(on_first, other_factor, factor)
    low = core * half
    first = lax.dynamic_slice_in_dim(first_state, low, half, 0)
    second = lax.dynamic_slice_in_dim(second_state, low, half, 0)
    first_factor = lax.dynamic_slice_in_dim(first_all, low, half, 0)
    second_factor = lax.dynamic_slice_in_dim(second_all, low, half, 0)
    chip_state = second_factor[:, None, None] * first + second
    chip_factor = first_factor * second_factor
    row_states, row_factors = unpacked(
        lax.all_gather(packed(chip_state, chip_factor), "cz"), width
    )
    total = jnp.zeros_like(chip_state)
    total_factor = jnp.ones_like(chip_factor)
    before = total
    before_factor = total_factor
    for z in range(row_states.shape[0]):
        here = z == row
        before = jnp.where(here, total, before)
        before_factor = jnp.where(here, total_factor, before_factor)
        total = row_factors[z][:, None, None] * total + row_states[z]
        total_factor = total_factor * row_factors[z]
    column_packed = lax.all_gather(packed(total, total_factor), "cy")
    column_packed, held = lax.optimization_barrier((column_packed, held))
    column_states, column_factors = unpacked(column_packed, width)
    above = jnp.zeros_like(chip_state)
    for y in range(column_states.shape[0]):
        joined = column_factors[y][:, None, None] * above + column_states[y]
        above = jnp.where(y < column, joined, above)
    prefix_half = before_factor[:, None, None] * above + before
    other_half = swapped(prefix_half)
    prefix = jnp.where(
        on_first,
        jnp.concatenate([prefix_half, other_half], axis=0),
        jnp.concatenate([other_half, prefix_half], axis=0),
    )
    later = first_all[:, None, None] * prefix + first_state
    return jnp.where(on_first, prefix, later), held


def linear_layer(linear_query, linear_key, linear_value, log_decay, norm_gain, held):
    length, columns = linear_query.shape
    heads = log_decay.shape[0]
    width = columns // heads
    blocks_here = length // BLK
    query_blocks = to_blocks(linear_query, heads)
    keys_blocks = to_blocks(linear_key, heads)
    values_blocks = to_blocks(linear_value, heads)
    per_block = log_decay.reshape(heads, blocks_here, BLK).transpose(1, 0, 2)
    cumulative = jnp.cumsum(per_block, axis=2)
    totals = cumulative[:, :, -1]
    section_cum = jnp.cumsum(log_decay, axis=1)
    section_total = section_cum[:, -1]
    carried = jnp.zeros((heads, width, width), jnp.float32)
    before = []
    for b in range(blocks_here):
        before.append(carried)
        carried = block_state(carried, keys_blocks[b], values_blocks[b], cumulative[b], totals[b])
    incoming, held = carry_in(carried, section_total, held)
    outputs = [
        block_output(before[b], query_blocks[b], keys_blocks[b], values_blocks[b], cumulative[b])
        for b in range(blocks_here)
    ]
    queries_flat = linear_query.reshape(length, heads, width)
    scaled = (queries_flat.astype(jnp.float32) * jnp.exp(section_cum).T[:, :, None]).astype(
        jnp.bfloat16
    )
    raw = jnp.concatenate(outputs, axis=0) + jnp.einsum(
        "thd,hde->the", scaled, incoming.astype(jnp.bfloat16), preferred_element_type=jnp.float32
    )
    square_mean = jnp.mean(raw * raw, axis=2, keepdims=True)
    normed = raw * lax.rsqrt(square_mean + EPS) * norm_gain.reshape(heads, width)
    return normed.astype(jnp.bfloat16).reshape(length, columns), held


def attend(query_blk, keys_sel, values_sel, allowed):
    width = query_blk.shape[-1]
    inverse_root = 1.0 / math.sqrt(width)
    scores = (
        jnp.einsum("thd,kjhd->htkj", query_blk, keys_sel, preferred_element_type=jnp.float32)
        * inverse_root
    )
    scores = jnp.where(allowed[None], scores, -jnp.inf)
    highest = jnp.max(scores, axis=(2, 3), keepdims=True)
    raised = jnp.exp(scores - highest)
    weights = (raised / jnp.sum(raised, axis=(2, 3), keepdims=True)).astype(jnp.bfloat16)
    output = jnp.einsum("htkj,kjhd->thd", weights, values_sel, preferred_element_type=jnp.float32)
    return output.astype(jnp.bfloat16)


def softmax_layer(soft_query, soft_key, soft_value, block_index, block_count, heads, sections):
    length, columns = soft_query.shape
    per_section = length // BLK
    slots = block_index.shape[1]
    own_pair = (soft_key, soft_value)
    farther = passed_along(own_pair, CTX, 2, sections)
    on_first = lax.axis_index("cc") == 0
    handed = jax.tree.map(lambda own, far: jnp.where(on_first, own, far), own_pair, farther)
    nearer = swapped(handed)
    pieces = [farther, nearer]
    window_key = jnp.concatenate([piece[0] for piece in pieces] + [soft_key], axis=0)
    window_value = jnp.concatenate([piece[1] for piece in pieces] + [soft_value], axis=0)
    key_blocks = to_blocks(window_key, heads)
    value_blocks = to_blocks(window_value, heads)
    section = lax.axis_index(CTX)
    first_block = (section - WIN_SEC) * per_section
    query_blocks = to_blocks(soft_query, heads)
    causal = causal_mask(BLK)
    slot_ids = jnp.arange(slots, dtype=jnp.int32)
    outputs = []
    for b in range(per_section):
        row_global = section * per_section + b
        low = b + WIN_SEC * per_section - (slots - 1)
        candidates = first_block + low + jnp.arange(slots, dtype=jnp.int32)
        used = slot_ids < block_count[b]
        matches = (block_index[b][None, :] == candidates[:, None]) & used[None, :]
        named = jnp.any(matches, axis=1)
        off_diagonal = candidates != row_global
        allowed = named[None, :, None] & (off_diagonal[None, :, None] | causal[:, None, :])
        outputs.append(
            attend(
                query_blocks[b],
                key_blocks[low : low + slots],
                value_blocks[low : low + slots],
                allowed,
            )
        )
    return jnp.concatenate(outputs, axis=0).reshape(length, columns)


def local(
    linear_query,
    linear_key,
    linear_value,
    log_decay,
    norm_gain,
    soft_query,
    soft_key,
    soft_value,
    block_index,
    block_count,
):
    heads = log_decay.shape[0]
    sections = lax.psum(1, CTX)
    softmax_heads = softmax_layer(
        soft_query, soft_key, soft_value, block_index, block_count, heads, sections
    )
    softmax_rows = lax.all_to_all(softmax_heads, "head", split_axis=0, concat_axis=1, tiled=True)
    linear_heads, softmax_rows = linear_layer(
        linear_query, linear_key, linear_value, log_decay, norm_gain, softmax_rows
    )
    linear_rows = lax.all_to_all(linear_heads, "head", split_axis=0, concat_axis=1, tiled=True)
    return (linear_rows, softmax_rows)


def solution(mesh):
    ctx, head = mesh.devices.shape
    split = mesh.devices.reshape(ctx // 16, 8, 2, head)
    mesh = jax.sharding.Mesh(split, CTX + ("head",))
    rows = P(CTX, "head")
    in_specs = (
        rows,
        rows,
        rows,
        P("head", CTX),
        P("head"),
        rows,
        rows,
        rows,
        P(CTX, None),
        P(CTX),
    )
    out_specs = (P(CTX + ("head",), None), P(CTX + ("head",), None))
    return jax.shard_map(local, mesh=mesh, in_specs=in_specs, out_specs=out_specs, check_vma=False)
```

```python
import math

import jax
import jax.numpy as jnp
from jax import lax
from jax.sharding import PartitionSpec as P

BLK = 128
WIN_SEC = 2


EPS = 1e-06


CTX = ("cy", "cz", "cc")


def passed_along(block, axis, distance, count):
    devices = range(count)
    route = [(i - distance, i) for i in devices if i - distance in devices]
    return lax.ppermute(block, axis, route)


def causal_mask(length):
    rows_iota = lax.broadcasted_iota(jnp.int32, (length, length), 0)
    cols_iota = lax.broadcasted_iota(jnp.int32, (length, length), 1)
    return cols_iota <= rows_iota


def to_blocks(matrix, heads):
    length, columns = matrix.shape
    return matrix.reshape(length // BLK, BLK, heads, columns // heads)


def block_state(carried, keys_blk, values_blk, cumul_blk, total_blk):
    factor = jnp.exp(total_blk[:, None] - cumul_blk).T
    decayed = (keys_blk.astype(jnp.float32) * factor[:, :, None]).astype(jnp.bfloat16)
    update = jnp.einsum("jhd,jhe->hde", decayed, values_blk, preferred_element_type=jnp.float32)
    return jnp.exp(total_blk)[:, None, None] * carried + update


def block_output(carried, query_blk, keys_blk, values_blk, cumul_blk):
    scores = jnp.einsum("thd,jhd->htj", query_blk, keys_blk, preferred_element_type=jnp.float32)
    differ = cumul_blk[:, :, None] - cumul_blk[:, None, :]
    allowed = causal_mask(query_blk.shape[0])
    weights = jnp.where(allowed[None], jnp.exp(jnp.minimum(differ, 0.0)), 0.0)
    mixing = (scores * weights).astype(jnp.bfloat16)
    inside = jnp.einsum("htj,jhd->thd", mixing, values_blk, preferred_element_type=jnp.float32)
    decayed_query = (query_blk.astype(jnp.float32) * jnp.exp(cumul_blk).T[:, :, None]).astype(
        jnp.bfloat16
    )
    across = jnp.einsum(
        "thd,hde->the",
        decayed_query,
        carried.astype(jnp.bfloat16),
        preferred_element_type=jnp.float32,
    )
    return inside + across


def packed(state, factor):
    heads, width, _ = state.shape
    return jnp.concatenate([state, jnp.broadcast_to(factor[:, None, None], (heads, 8, width))], axis=1)


def unpacked(both, width):
    return both[..., :width, :], both[..., width, 0]


def swapped(block):
    return lax.ppermute(block, "cc", [(0, 1), (1, 0)])


def carry_in(final, section_total, pair, between):
    heads, width, _ = final.shape
    half = heads // 2
    core, row, column = (lax.axis_index("cc"), lax.axis_index("cz"), lax.axis_index("cy"))
    factor = jnp.exp(section_total)
    other_state, other_factor = unpacked(swapped(packed(final, factor)), width)
    on_first = core == 0
    first_state = jnp.where(on_first, final, other_state)
    first_all = jnp.where(on_first, factor, other_factor)
    second_state = jnp.where(on_first, other_state, final)
    second_all = jnp.where(on_first, other_factor, factor)
    low = core * half
    first = lax.dynamic_slice_in_dim(first_state, low, half, 0)
    second = lax.dynamic_slice_in_dim(second_state, low, half, 0)
    first_factor = lax.dynamic_slice_in_dim(first_all, low, half, 0)
    second_factor = lax.dynamic_slice_in_dim(second_all, low, half, 0)
    chip_state = second_factor[:, None, None] * first + second
    chip_factor = first_factor * second_factor
    row_packed = lax.all_gather(packed(chip_state, chip_factor), "cz")
    row_packed, pair = lax.optimization_barrier((row_packed, pair))
    held = between(pair)
    row_states, row_factors = unpacked(row_packed, width)
    total = jnp.zeros_like(chip_state)
    total_factor = jnp.ones_like(chip_factor)
    before = total
    before_factor = total_factor
    for z in range(row_states.shape[0]):
        here = z == row
        before = jnp.where(here, total, before)
        before_factor = jnp.where(here, total_factor, before_factor)
        total = row_factors[z][:, None, None] * total + row_states[z]
        total_factor = total_factor * row_factors[z]
    column_packed = lax.all_gather(packed(total, total_factor), "cy")
    column_packed, held = lax.optimization_barrier((column_packed, held))
    column_states, column_factors = unpacked(column_packed, width)
    above = jnp.zeros_like(chip_state)
    for y in range(column_states.shape[0]):
        joined = column_factors[y][:, None, None] * above + column_states[y]
        above = jnp.where(y < column, joined, above)
    prefix_half = before_factor[:, None, None] * above + before
    other_half = swapped(prefix_half)
    prefix = jnp.where(
        on_first,
        jnp.concatenate([prefix_half, other_half], axis=0),
        jnp.concatenate([other_half, prefix_half], axis=0),
    )
    later = first_all[:, None, None] * prefix + first_state
    return jnp.where(on_first, prefix, later), held


def linear_layer(linear_query, linear_key, linear_value, log_decay, norm_gain, pair, between):
    length, columns = linear_query.shape
    heads = log_decay.shape[0]
    width = columns // heads
    blocks_here = length // BLK
    query_blocks = to_blocks(linear_query, heads)
    keys_blocks = to_blocks(linear_key, heads)
    values_blocks = to_blocks(linear_value, heads)
    per_block = log_decay.reshape(heads, blocks_here, BLK).transpose(1, 0, 2)
    cumulative = jnp.cumsum(per_block, axis=2)
    totals = cumulative[:, :, -1]
    section_cum = jnp.cumsum(log_decay, axis=1)
    section_total = section_cum[:, -1]
    carried = jnp.zeros((heads, width, width), jnp.float32)
    before = []
    for b in range(blocks_here):
        before.append(carried)
        carried = block_state(carried, keys_blocks[b], values_blocks[b], cumulative[b], totals[b])
    incoming, held = carry_in(carried, section_total, pair, between)
    outputs = [
        block_output(before[b], query_blocks[b], keys_blocks[b], values_blocks[b], cumulative[b])
        for b in range(blocks_here)
    ]
    queries_flat = linear_query.reshape(length, heads, width)
    scaled = (queries_flat.astype(jnp.float32) * jnp.exp(section_cum).T[:, :, None]).astype(
        jnp.bfloat16
    )
    raw = jnp.concatenate(outputs, axis=0) + jnp.einsum(
        "thd,hde->the", scaled, incoming.astype(jnp.bfloat16), preferred_element_type=jnp.float32
    )
    square_mean = jnp.mean(raw * raw, axis=2, keepdims=True)
    normed = raw * lax.rsqrt(square_mean + EPS) * norm_gain.reshape(heads, width)
    return normed.astype(jnp.bfloat16).reshape(length, columns), held


def attend(query_blk, keys_sel, values_sel, allowed):
    width = query_blk.shape[-1]
    inverse_root = 1.0 / math.sqrt(width)
    scores = (
        jnp.einsum("thd,kjhd->htkj", query_blk, keys_sel, preferred_element_type=jnp.float32)
        * inverse_root
    )
    scores = jnp.where(allowed[None], scores, -jnp.inf)
    highest = jnp.max(scores, axis=(2, 3), keepdims=True)
    raised = jnp.exp(scores - highest)
    weights = (raised / jnp.sum(raised, axis=(2, 3), keepdims=True)).astype(jnp.bfloat16)
    output = jnp.einsum("htkj,kjhd->thd", weights, values_sel, preferred_element_type=jnp.float32)
    return output.astype(jnp.bfloat16)


def softmax_layer(soft_query, soft_key, soft_value, block_index, block_count, heads, sections):
    length, columns = soft_query.shape
    per_section = length // BLK
    slots = block_index.shape[1]
    own_pair = (soft_key, soft_value)
    farther = passed_along(own_pair, CTX, 2, sections)
    on_first = lax.axis_index("cc") == 0
    handed = jax.tree.map(lambda own, far: jnp.where(on_first, own, far), own_pair, farther)
    nearer = swapped(handed)
    pieces = [farther, nearer]
    window_key = jnp.concatenate([piece[0] for piece in pieces] + [soft_key], axis=0)
    window_value = jnp.concatenate([piece[1] for piece in pieces] + [soft_value], axis=0)
    key_blocks = to_blocks(window_key, heads)
    value_blocks = to_blocks(window_value, heads)
    section = lax.axis_index(CTX)
    first_block = (section - WIN_SEC) * per_section
    query_blocks = to_blocks(soft_query, heads)
    causal = causal_mask(BLK)
    slot_ids = jnp.arange(slots, dtype=jnp.int32)
    outputs = []
    for b in range(per_section):
        row_global = section * per_section + b
        low = b + WIN_SEC * per_section - (slots - 1)
        candidates = first_block + low + jnp.arange(slots, dtype=jnp.int32)
        used = slot_ids < block_count[b]
        matches = (block_index[b][None, :] == candidates[:, None]) & used[None, :]
        named = jnp.any(matches, axis=1)
        off_diagonal = candidates != row_global
        allowed = named[None, :, None] & (off_diagonal[None, :, None] | causal[:, None, :])
        outputs.append(
            attend(
                query_blocks[b],
                key_blocks[low : low + slots],
                value_blocks[low : low + slots],
                allowed,
            )
        )
    return jnp.concatenate(outputs, axis=0).reshape(length, columns)


def local(
    linear_query,
    linear_key,
    linear_value,
    log_decay,
    norm_gain,
    soft_query,
    soft_key,
    soft_value,
    block_index,
    block_count,
):
    heads = log_decay.shape[0]
    sections = lax.psum(1, CTX)

    def between(pair):
        softmax_heads = softmax_layer(
            soft_query, pair[0], pair[1], block_index, block_count, heads, sections
        )
        return lax.all_to_all(softmax_heads, "head", split_axis=0, concat_axis=1, tiled=True)

    linear_heads, softmax_rows = linear_layer(
        linear_query, linear_key, linear_value, log_decay, norm_gain, (soft_key, soft_value), between
    )
    linear_rows = lax.all_to_all(linear_heads, "head", split_axis=0, concat_axis=1, tiled=True)
    return (linear_rows, softmax_rows)


def solution(mesh):
    ctx, head = mesh.devices.shape
    split = mesh.devices.reshape(ctx // 16, 8, 2, head)
    mesh = jax.sharding.Mesh(split, CTX + ("head",))
    rows = P(CTX, "head")
    in_specs = (
        rows,
        rows,
        rows,
        P("head", CTX),
        P("head"),
        rows,
        rows,
        rows,
        P(CTX, None),
        P(CTX),
    )
    out_specs = (P(CTX + ("head",), None), P(CTX + ("head",), None))
    return jax.shard_map(local, mesh=mesh, in_specs=in_specs, out_specs=out_specs, check_vma=False)
```

```python
import math

import jax
import jax.numpy as jnp
from jax import lax
from jax.sharding import PartitionSpec as P

BLK = 128
WIN_SEC = 2


EPS = 1e-06


CTX = ("cy", "cz", "cc")


def passed_along(block, axis, distance, count):
    devices = range(count)
    route = [(i - distance, i) for i in devices if i - distance in devices]
    return lax.ppermute(block, axis, route)


def causal_mask(length):
    rows_iota = lax.broadcasted_iota(jnp.int32, (length, length), 0)
    cols_iota = lax.broadcasted_iota(jnp.int32, (length, length), 1)
    return cols_iota <= rows_iota


def to_blocks(matrix, heads):
    length, columns = matrix.shape
    return matrix.reshape(length // BLK, BLK, heads, columns // heads)


def block_state(carried, keys_blk, values_blk, cumul_blk, total_blk):
    factor = jnp.exp(total_blk[:, None] - cumul_blk).T
    decayed = (keys_blk.astype(jnp.float32) * factor[:, :, None]).astype(jnp.bfloat16)
    update = jnp.einsum("jhd,jhe->hde", decayed, values_blk, preferred_element_type=jnp.float32)
    return jnp.exp(total_blk)[:, None, None] * carried + update


def block_output(carried, query_blk, keys_blk, values_blk, cumul_blk):
    scores = jnp.einsum("thd,jhd->htj", query_blk, keys_blk, preferred_element_type=jnp.float32)
    differ = cumul_blk[:, :, None] - cumul_blk[:, None, :]
    allowed = causal_mask(query_blk.shape[0])
    weights = jnp.where(allowed[None], jnp.exp(jnp.minimum(differ, 0.0)), 0.0)
    mixing = (scores * weights).astype(jnp.bfloat16)
    inside = jnp.einsum("htj,jhd->thd", mixing, values_blk, preferred_element_type=jnp.float32)
    decayed_query = (query_blk.astype(jnp.float32) * jnp.exp(cumul_blk).T[:, :, None]).astype(
        jnp.bfloat16
    )
    across = jnp.einsum(
        "thd,hde->the",
        decayed_query,
        carried.astype(jnp.bfloat16),
        preferred_element_type=jnp.float32,
    )
    return inside + across


def packed(state, factor):
    heads, width, _ = state.shape
    return jnp.concatenate([state, jnp.broadcast_to(factor[:, None, None], (heads, 8, width))], axis=1)


def unpacked(both, width):
    return both[..., :width, :], both[..., width, 0]


def narrow(state, factor):
    heads, width, _ = state.shape
    high = factor.astype(jnp.bfloat16)
    low = (factor - high.astype(jnp.float32)).astype(jnp.bfloat16)
    rows = lambda part: jnp.broadcast_to(part[:, None, None], (heads, 8, width))
    return jnp.concatenate([state.astype(jnp.bfloat16), rows(high), rows(low)], axis=1)


def widened(both, width):
    wide = both.astype(jnp.float32)
    return wide[..., :width, :], wide[..., width, 0] + wide[..., width + 8, 0]


def folded(states, factors, upto):
    places = jnp.arange(states.shape[0])
    between = (places[:, None] < places[None, :]) & (places[None, :] < upto)
    weights = jnp.prod(jnp.where(between[:, :, None], factors[None], 1.0), axis=1)
    weights = jnp.where((places < upto)[:, None], weights, 0.0)
    return jnp.sum(weights[:, :, None, None] * states, axis=0)


def spanned(factors, upto):
    places = jnp.arange(factors.shape[0])
    return jnp.prod(jnp.where((places < upto)[:, None], factors, 1.0), axis=0)


def swapped(block):
    return lax.ppermute(block, "cc", [(0, 1), (1, 0)])


def carry_in(final, section_total, held):
    heads, width, _ = final.shape
    half = heads // 2
    core, row, column = (lax.axis_index("cc"), lax.axis_index("cz"), lax.axis_index("cy"))
    factor = jnp.exp(section_total)
    other_state, other_factor = unpacked(swapped(packed(final, factor)), width)
    on_first = core == 0
    first_state = jnp.where(on_first, final, other_state)
    first_all = jnp.where(on_first, factor, other_factor)
    second_state = jnp.where(on_first, other_state, final)
    second_all = jnp.where(on_first, other_factor, factor)
    low = core * half
    first = lax.dynamic_slice_in_dim(first_state, low, half, 0)
    second = lax.dynamic_slice_in_dim(second_state, low, half, 0)
    first_factor = lax.dynamic_slice_in_dim(first_all, low, half, 0)
    second_factor = lax.dynamic_slice_in_dim(second_all, low, half, 0)
    chip_state = second_factor[:, None, None] * first + second
    chip_factor = first_factor * second_factor
    row_states, row_factors = widened(
        lax.all_gather(narrow(chip_state, chip_factor), "cz"), width
    )
    count = row_states.shape[0]
    before = folded(row_states, row_factors, row)
    before_factor = spanned(row_factors, row)
    total = folded(row_states, row_factors, count)
    total_factor = spanned(row_factors, count)
    column_packed = lax.all_gather(narrow(total, total_factor), "cy")
    column_packed, held = lax.optimization_barrier((column_packed, held))
    column_states, column_factors = widened(column_packed, width)
    above = folded(column_states, column_factors, column)
    prefix_half = before_factor[:, None, None] * above + before
    other_half = swapped(prefix_half)
    prefix = jnp.where(
        on_first,
        jnp.concatenate([prefix_half, other_half], axis=0),
        jnp.concatenate([other_half, prefix_half], axis=0),
    )
    later = first_all[:, None, None] * prefix + first_state
    return jnp.where(on_first, prefix, later), held


def linear_layer(linear_query, linear_key, linear_value, log_decay, norm_gain, held):
    length, columns = linear_query.shape
    heads = log_decay.shape[0]
    width = columns // heads
    blocks_here = length // BLK
    query_blocks = to_blocks(linear_query, heads)
    keys_blocks = to_blocks(linear_key, heads)
    values_blocks = to_blocks(linear_value, heads)
    per_block = log_decay.reshape(heads, blocks_here, BLK).transpose(1, 0, 2)
    cumulative = jnp.cumsum(per_block, axis=2)
    totals = cumulative[:, :, -1]
    section_cum = jnp.cumsum(log_decay, axis=1)
    section_total = section_cum[:, -1]
    carried = jnp.zeros((heads, width, width), jnp.float32)
    before = []
    for b in range(blocks_here):
        before.append(carried)
        carried = block_state(carried, keys_blocks[b], values_blocks[b], cumulative[b], totals[b])
    incoming, held = carry_in(carried, section_total, held)
    outputs = [
        block_output(before[b], query_blocks[b], keys_blocks[b], values_blocks[b], cumulative[b])
        for b in range(blocks_here)
    ]
    queries_flat = linear_query.reshape(length, heads, width)
    scaled = (queries_flat.astype(jnp.float32) * jnp.exp(section_cum).T[:, :, None]).astype(
        jnp.bfloat16
    )
    raw = jnp.concatenate(outputs, axis=0) + jnp.einsum(
        "thd,hde->the", scaled, incoming.astype(jnp.bfloat16), preferred_element_type=jnp.float32
    )
    square_mean = jnp.mean(raw * raw, axis=2, keepdims=True)
    normed = raw * lax.rsqrt(square_mean + EPS) * norm_gain.reshape(heads, width)
    return normed.astype(jnp.bfloat16).reshape(length, columns), held


def attend(query_blk, keys_sel, values_sel, allowed):
    width = query_blk.shape[-1]
    inverse_root = 1.0 / math.sqrt(width)
    scores = (
        jnp.einsum("thd,kjhd->htkj", query_blk, keys_sel, preferred_element_type=jnp.float32)
        * inverse_root
    )
    scores = jnp.where(allowed[None], scores, -jnp.inf)
    highest = jnp.max(scores, axis=(2, 3), keepdims=True)
    raised = jnp.exp(scores - highest)
    weights = (raised / jnp.sum(raised, axis=(2, 3), keepdims=True)).astype(jnp.bfloat16)
    output = jnp.einsum("htkj,kjhd->thd", weights, values_sel, preferred_element_type=jnp.float32)
    return output.astype(jnp.bfloat16)


def softmax_layer(soft_query, soft_key, soft_value, block_index, block_count, heads, sections):
    length, columns = soft_query.shape
    per_section = length // BLK
    slots = block_index.shape[1]
    own_pair = (soft_key, soft_value)
    farther = passed_along(own_pair, CTX, 2, sections)
    on_first = lax.axis_index("cc") == 0
    handed = jax.tree.map(lambda own, far: jnp.where(on_first, own, far), own_pair, farther)
    nearer = swapped(handed)
    pieces = [farther, nearer]
    window_key = jnp.concatenate([piece[0] for piece in pieces] + [soft_key], axis=0)
    window_value = jnp.concatenate([piece[1] for piece in pieces] + [soft_value], axis=0)
    key_blocks = to_blocks(window_key, heads)
    value_blocks = to_blocks(window_value, heads)
    section = lax.axis_index(CTX)
    first_block = (section - WIN_SEC) * per_section
    query_blocks = to_blocks(soft_query, heads)
    causal = causal_mask(BLK)
    slot_ids = jnp.arange(slots, dtype=jnp.int32)
    outputs = []
    for b in range(per_section):
        row_global = section * per_section + b
        low = b + WIN_SEC * per_section - (slots - 1)
        candidates = first_block + low + jnp.arange(slots, dtype=jnp.int32)
        used = slot_ids < block_count[b]
        matches = (block_index[b][None, :] == candidates[:, None]) & used[None, :]
        named = jnp.any(matches, axis=1)
        off_diagonal = candidates != row_global
        allowed = named[None, :, None] & (off_diagonal[None, :, None] | causal[:, None, :])
        outputs.append(
            attend(
                query_blocks[b],
                key_blocks[low : low + slots],
                value_blocks[low : low + slots],
                allowed,
            )
        )
    return jnp.concatenate(outputs, axis=0).reshape(length, columns)


def local(
    linear_query,
    linear_key,
    linear_value,
    log_decay,
    norm_gain,
    soft_query,
    soft_key,
    soft_value,
    block_index,
    block_count,
):
    heads = log_decay.shape[0]
    sections = lax.psum(1, CTX)
    softmax_heads = softmax_layer(
        soft_query, soft_key, soft_value, block_index, block_count, heads, sections
    )
    softmax_rows = lax.all_to_all(softmax_heads, "head", split_axis=0, concat_axis=1, tiled=True)
    linear_heads, softmax_rows = linear_layer(
        linear_query, linear_key, linear_value, log_decay, norm_gain, softmax_rows
    )
    linear_rows = lax.all_to_all(linear_heads, "head", split_axis=0, concat_axis=1, tiled=True)
    return (linear_rows, softmax_rows)


def solution(mesh):
    ctx, head = mesh.devices.shape
    split = mesh.devices.reshape(ctx // 16, 8, 2, head)
    mesh = jax.sharding.Mesh(split, CTX + ("head",))
    rows = P(CTX, "head")
    in_specs = (
        rows,
        rows,
        rows,
        P("head", CTX),
        P("head"),
        rows,
        rows,
        rows,
        P(CTX, None),
        P(CTX),
    )
    out_specs = (P(CTX + ("head",), None), P(CTX + ("head",), None))
    return jax.shard_map(local, mesh=mesh, in_specs=in_specs, out_specs=out_specs, check_vma=False)
```

```python
import math

import jax
import jax.numpy as jnp
from jax import lax
from jax.sharding import PartitionSpec as P

BLK = 128
WIN_SEC = 2


EPS = 1e-06


CTX = ("cy", "cz", "cc")


def passed_along(block, axis, distance, count):
    devices = range(count)
    route = [(i - distance, i) for i in devices if i - distance in devices]
    return lax.ppermute(block, axis, route)


def causal_mask(length):
    rows_iota = lax.broadcasted_iota(jnp.int32, (length, length), 0)
    cols_iota = lax.broadcasted_iota(jnp.int32, (length, length), 1)
    return cols_iota <= rows_iota


def to_blocks(matrix, heads):
    length, columns = matrix.shape
    return matrix.reshape(length // BLK, BLK, heads, columns // heads)


def block_state(carried, keys_blk, values_blk, cumul_blk, total_blk):
    factor = jnp.exp(total_blk[:, None] - cumul_blk).T
    decayed = (keys_blk.astype(jnp.float32) * factor[:, :, None]).astype(jnp.bfloat16)
    update = jnp.einsum("jhd,jhe->hde", decayed, values_blk, preferred_element_type=jnp.float32)
    return jnp.exp(total_blk)[:, None, None] * carried + update


def block_output(carried, query_blk, keys_blk, values_blk, cumul_blk):
    scores = jnp.einsum("thd,jhd->htj", query_blk, keys_blk, preferred_element_type=jnp.float32)
    differ = cumul_blk[:, :, None] - cumul_blk[:, None, :]
    allowed = causal_mask(query_blk.shape[0])
    weights = jnp.where(allowed[None], jnp.exp(jnp.minimum(differ, 0.0)), 0.0)
    mixing = (scores * weights).astype(jnp.bfloat16)
    inside = jnp.einsum("htj,jhd->thd", mixing, values_blk, preferred_element_type=jnp.float32)
    decayed_query = (query_blk.astype(jnp.float32) * jnp.exp(cumul_blk).T[:, :, None]).astype(
        jnp.bfloat16
    )
    across = jnp.einsum(
        "thd,hde->the",
        decayed_query,
        carried.astype(jnp.bfloat16),
        preferred_element_type=jnp.float32,
    )
    return inside + across


def packed(state, factor):
    heads, width, _ = state.shape
    return jnp.concatenate([state, jnp.broadcast_to(factor[:, None, None], (heads, 8, width))], axis=1)


def unpacked(both, width):
    return both[..., :width, :], both[..., width, 0]


def folded(states, factors, upto):
    places = jnp.arange(states.shape[0])
    between = (places[:, None] < places[None, :]) & (places[None, :] < upto)
    weights = jnp.prod(jnp.where(between[:, :, None], factors[None], 1.0), axis=1)
    weights = jnp.where((places < upto)[:, None], weights, 0.0)
    return jnp.sum(weights[:, :, None, None] * states, axis=0)


def spanned(factors, upto):
    places = jnp.arange(factors.shape[0])
    return jnp.prod(jnp.where((places < upto)[:, None], factors, 1.0), axis=0)


def swapped(block):
    return lax.ppermute(block, "cc", [(0, 1), (1, 0)])


def carry_in(final, section_total, held):
    heads, width, _ = final.shape
    half = heads // 2
    core, row, column = (lax.axis_index("cc"), lax.axis_index("cz"), lax.axis_index("cy"))
    factor = jnp.exp(section_total)
    other_state, other_factor = unpacked(swapped(packed(final, factor)), width)
    on_first = core == 0
    first_state = jnp.where(on_first, final, other_state)
    first_all = jnp.where(on_first, factor, other_factor)
    second_state = jnp.where(on_first, other_state, final)
    second_all = jnp.where(on_first, other_factor, factor)
    low = core * half
    first = lax.dynamic_slice_in_dim(first_state, low, half, 0)
    second = lax.dynamic_slice_in_dim(second_state, low, half, 0)
    first_factor = lax.dynamic_slice_in_dim(first_all, low, half, 0)
    second_factor = lax.dynamic_slice_in_dim(second_all, low, half, 0)
    chip_state = second_factor[:, None, None] * first + second
    chip_factor = first_factor * second_factor
    row_states, row_factors = unpacked(
        lax.all_gather(packed(chip_state, chip_factor), "cz"), width
    )
    count = row_states.shape[0]
    before = folded(row_states, row_factors, row)
    before_factor = spanned(row_factors, row)
    total = folded(row_states, row_factors, count)
    total_factor = spanned(row_factors, count)
    column_packed = lax.all_gather(packed(total, total_factor), "cy")
    column_packed, held = lax.optimization_barrier((column_packed, held))
    column_states, column_factors = unpacked(column_packed, width)
    above = folded(column_states, column_factors, column)
    prefix_half = before_factor[:, None, None] * above + before
    other_half = swapped(prefix_half)
    prefix = jnp.where(
        on_first,
        jnp.concatenate([prefix_half, other_half], axis=0),
        jnp.concatenate([other_half, prefix_half], axis=0),
    )
    later = first_all[:, None, None] * prefix + first_state
    return jnp.where(on_first, prefix, later), held


def linear_layer(linear_query, linear_key, linear_value, log_decay, norm_gain, held):
    length, columns = linear_query.shape
    heads = log_decay.shape[0]
    width = columns // heads
    blocks_here = length // BLK
    query_blocks = to_blocks(linear_query, heads)
    keys_blocks = to_blocks(linear_key, heads)
    values_blocks = to_blocks(linear_value, heads)
    per_block = log_decay.reshape(heads, blocks_here, BLK).transpose(1, 0, 2)
    cumulative = jnp.cumsum(per_block, axis=2)
    totals = cumulative[:, :, -1]
    section_cum = jnp.cumsum(log_decay, axis=1)
    section_total = section_cum[:, -1]
    carried = jnp.zeros((heads, width, width), jnp.float32)
    before = []
    for b in range(blocks_here):
        before.append(carried)
        carried = block_state(carried, keys_blocks[b], values_blocks[b], cumulative[b], totals[b])
    incoming, held = carry_in(carried, section_total, held)
    outputs = [
        block_output(before[b], query_blocks[b], keys_blocks[b], values_blocks[b], cumulative[b])
        for b in range(blocks_here)
    ]
    queries_flat = linear_query.reshape(length, heads, width)
    scaled = (queries_flat.astype(jnp.float32) * jnp.exp(section_cum).T[:, :, None]).astype(
        jnp.bfloat16
    )
    raw = jnp.concatenate(outputs, axis=0) + jnp.einsum(
        "thd,hde->the", scaled, incoming.astype(jnp.bfloat16), preferred_element_type=jnp.float32
    )
    square_mean = jnp.mean(raw * raw, axis=2, keepdims=True)
    normed = raw * lax.rsqrt(square_mean + EPS) * norm_gain.reshape(heads, width)
    return normed.astype(jnp.bfloat16).reshape(length, columns), held


def attend(query_blk, keys_sel, values_sel, allowed):
    width = query_blk.shape[-1]
    inverse_root = 1.0 / math.sqrt(width)
    scores = (
        jnp.einsum("thd,kjhd->htkj", query_blk, keys_sel, preferred_element_type=jnp.float32)
        * inverse_root
    )
    scores = jnp.where(allowed[None], scores, -jnp.inf)
    highest = jnp.max(scores, axis=(2, 3), keepdims=True)
    raised = jnp.exp(scores - highest)
    weights = (raised / jnp.sum(raised, axis=(2, 3), keepdims=True)).astype(jnp.bfloat16)
    output = jnp.einsum("htkj,kjhd->thd", weights, values_sel, preferred_element_type=jnp.float32)
    return output.astype(jnp.bfloat16)


def softmax_layer(soft_query, soft_key, soft_value, block_index, block_count, heads, sections):
    length, columns = soft_query.shape
    per_section = length // BLK
    slots = block_index.shape[1]
    own_pair = (soft_key, soft_value)
    farther = passed_along(own_pair, CTX, 2, sections)
    on_first = lax.axis_index("cc") == 0
    handed = jax.tree.map(lambda own, far: jnp.where(on_first, own, far), own_pair, farther)
    nearer = swapped(handed)
    pieces = [farther, nearer]
    window_key = jnp.concatenate([piece[0] for piece in pieces] + [soft_key], axis=0)
    window_value = jnp.concatenate([piece[1] for piece in pieces] + [soft_value], axis=0)
    key_blocks = to_blocks(window_key, heads)
    value_blocks = to_blocks(window_value, heads)
    section = lax.axis_index(CTX)
    first_block = (section - WIN_SEC) * per_section
    query_blocks = to_blocks(soft_query, heads)
    causal = causal_mask(BLK)
    slot_ids = jnp.arange(slots, dtype=jnp.int32)
    outputs = []
    for b in range(per_section):
        row_global = section * per_section + b
        low = b + WIN_SEC * per_section - (slots - 1)
        candidates = first_block + low + jnp.arange(slots, dtype=jnp.int32)
        used = slot_ids < block_count[b]
        matches = (block_index[b][None, :] == candidates[:, None]) & used[None, :]
        named = jnp.any(matches, axis=1)
        off_diagonal = candidates != row_global
        allowed = named[None, :, None] & (off_diagonal[None, :, None] | causal[:, None, :])
        outputs.append(
            attend(
                query_blocks[b],
                key_blocks[low : low + slots],
                value_blocks[low : low + slots],
                allowed,
            )
        )
    return jnp.concatenate(outputs, axis=0).reshape(length, columns)


def local(
    linear_query,
    linear_key,
    linear_value,
    log_decay,
    norm_gain,
    soft_query,
    soft_key,
    soft_value,
    block_index,
    block_count,
):
    heads = log_decay.shape[0]
    sections = lax.psum(1, CTX)
    softmax_heads = softmax_layer(
        soft_query, soft_key, soft_value, block_index, block_count, heads, sections
    )
    softmax_rows = lax.all_to_all(softmax_heads, "head", split_axis=0, concat_axis=1, tiled=True)
    linear_heads, softmax_rows = linear_layer(
        linear_query, linear_key, linear_value, log_decay, norm_gain, softmax_rows
    )
    linear_rows = lax.all_to_all(linear_heads, "head", split_axis=0, concat_axis=1, tiled=True)
    return (linear_rows, softmax_rows)


def solution(mesh):
    ctx, head = mesh.devices.shape
    split = mesh.devices.reshape(ctx // 16, 8, 2, head)
    mesh = jax.sharding.Mesh(split, CTX + ("head",))
    rows = P(CTX, "head")
    in_specs = (
        rows,
        rows,
        rows,
        P("head", CTX),
        P("head"),
        rows,
        rows,
        rows,
        P(CTX, None),
        P(CTX),
    )
    out_specs = (P(CTX + ("head",), None), P(CTX + ("head",), None))
    return jax.shard_map(local, mesh=mesh, in_specs=in_specs, out_specs=out_specs, check_vma=False)
```

```python
import math

import jax
import jax.numpy as jnp
from jax import lax
from jax.sharding import PartitionSpec as P

BLK = 128
WIN_SEC = 2


EPS = 1e-06


CTX = ("cy", "cz", "cc")


def passed_along(block, axis, distance, count):
    devices = range(count)
    route = [(i - distance, i) for i in devices if i - distance in devices]
    return lax.ppermute(block, axis, route)


def causal_mask(length):
    rows_iota = lax.broadcasted_iota(jnp.int32, (length, length), 0)
    cols_iota = lax.broadcasted_iota(jnp.int32, (length, length), 1)
    return cols_iota <= rows_iota


def to_blocks(matrix, heads):
    length, columns = matrix.shape
    return matrix.reshape(length // BLK, BLK, heads, columns // heads)


def block_state(carried, keys_blk, values_blk, cumul_blk, total_blk):
    factor = jnp.exp(total_blk[:, None] - cumul_blk).T
    decayed = (keys_blk.astype(jnp.float32) * factor[:, :, None]).astype(jnp.bfloat16)
    update = jnp.einsum("jhd,jhe->hde", decayed, values_blk, preferred_element_type=jnp.float32)
    return jnp.exp(total_blk)[:, None, None] * carried + update


def block_output(carried, query_blk, keys_blk, values_blk, cumul_blk):
    scores = jnp.einsum("thd,jhd->htj", query_blk, keys_blk, preferred_element_type=jnp.float32)
    differ = cumul_blk[:, :, None] - cumul_blk[:, None, :]
    allowed = causal_mask(query_blk.shape[0])
    weights = jnp.where(allowed[None], jnp.exp(jnp.minimum(differ, 0.0)), 0.0)
    mixing = (scores * weights).astype(jnp.bfloat16)
    inside = jnp.einsum("htj,jhd->thd", mixing, values_blk, preferred_element_type=jnp.float32)
    decayed_query = (query_blk.astype(jnp.float32) * jnp.exp(cumul_blk).T[:, :, None]).astype(
        jnp.bfloat16
    )
    across = jnp.einsum(
        "thd,hde->the",
        decayed_query,
        carried.astype(jnp.bfloat16),
        preferred_element_type=jnp.float32,
    )
    return inside + across


def packed(state, factor):
    heads, width, _ = state.shape
    return jnp.concatenate([state, jnp.broadcast_to(factor[:, None, None], (heads, 8, width))], axis=1)


def unpacked(both, width):
    return both[..., :width, :], both[..., width, 0]


def narrow(state, factor):
    heads, width, _ = state.shape
    high = factor.astype(jnp.bfloat16)
    low = (factor - high.astype(jnp.float32)).astype(jnp.bfloat16)
    rows = lambda part: jnp.broadcast_to(part[:, None, None], (heads, 8, width))
    return jnp.concatenate([state.astype(jnp.bfloat16), rows(high), rows(low)], axis=1)


def widened(both, width):
    wide = both.astype(jnp.float32)
    return wide[..., :width, :], wide[..., width, 0] + wide[..., width + 8, 0]


def folded(states, factors, upto):
    places = jnp.arange(states.shape[0])
    between = (places[:, None] < places[None, :]) & (places[None, :] < upto)
    weights = jnp.prod(jnp.where(between[:, :, None], factors[None], 1.0), axis=1)
    weights = jnp.where((places < upto)[:, None], weights, 0.0)
    return jnp.sum(weights[:, :, None, None] * states, axis=0)


def spanned(factors, upto):
    places = jnp.arange(factors.shape[0])
    return jnp.prod(jnp.where((places < upto)[:, None], factors, 1.0), axis=0)


def swapped(block):
    return lax.ppermute(block, "cc", [(0, 1), (1, 0)])


def carry_in(final, section_total, held):
    heads, width, _ = final.shape
    half = heads // 2
    core, row, column = (lax.axis_index("cc"), lax.axis_index("cz"), lax.axis_index("cy"))
    factor = jnp.exp(section_total)
    other_state, other_factor = unpacked(swapped(packed(final, factor)), width)
    on_first = core == 0
    first_state = jnp.where(on_first, final, other_state)
    first_all = jnp.where(on_first, factor, other_factor)
    second_state = jnp.where(on_first, other_state, final)
    second_all = jnp.where(on_first, other_factor, factor)
    low = core * half
    first = lax.dynamic_slice_in_dim(first_state, low, half, 0)
    second = lax.dynamic_slice_in_dim(second_state, low, half, 0)
    first_factor = lax.dynamic_slice_in_dim(first_all, low, half, 0)
    second_factor = lax.dynamic_slice_in_dim(second_all, low, half, 0)
    chip_state = second_factor[:, None, None] * first + second
    chip_factor = first_factor * second_factor
    row_states, row_factors = widened(
        lax.all_gather(narrow(chip_state, chip_factor), "cz"), width
    )
    count = row_states.shape[0]
    before = folded(row_states, row_factors, row)
    before_factor = spanned(row_factors, row)
    total = folded(row_states, row_factors, count)
    total_factor = spanned(row_factors, count)
    column_packed = lax.all_gather(packed(total, total_factor), "cy")
    column_packed, held = lax.optimization_barrier((column_packed, held))
    column_states, column_factors = unpacked(column_packed, width)
    above = folded(column_states, column_factors, column)
    prefix_half = before_factor[:, None, None] * above + before
    other_half = swapped(prefix_half)
    prefix = jnp.where(
        on_first,
        jnp.concatenate([prefix_half, other_half], axis=0),
        jnp.concatenate([other_half, prefix_half], axis=0),
    )
    later = first_all[:, None, None] * prefix + first_state
    return jnp.where(on_first, prefix, later), held


def linear_layer(linear_query, linear_key, linear_value, log_decay, norm_gain, held):
    length, columns = linear_query.shape
    heads = log_decay.shape[0]
    width = columns // heads
    blocks_here = length // BLK
    query_blocks = to_blocks(linear_query, heads)
    keys_blocks = to_blocks(linear_key, heads)
    values_blocks = to_blocks(linear_value, heads)
    per_block = log_decay.reshape(heads, blocks_here, BLK).transpose(1, 0, 2)
    cumulative = jnp.cumsum(per_block, axis=2)
    totals = cumulative[:, :, -1]
    section_cum = jnp.cumsum(log_decay, axis=1)
    section_total = section_cum[:, -1]
    carried = jnp.zeros((heads, width, width), jnp.float32)
    before = []
    for b in range(blocks_here):
        before.append(carried)
        carried = block_state(carried, keys_blocks[b], values_blocks[b], cumulative[b], totals[b])
    incoming, held = carry_in(carried, section_total, held)
    outputs = [
        block_output(before[b], query_blocks[b], keys_blocks[b], values_blocks[b], cumulative[b])
        for b in range(blocks_here)
    ]
    queries_flat = linear_query.reshape(length, heads, width)
    scaled = (queries_flat.astype(jnp.float32) * jnp.exp(section_cum).T[:, :, None]).astype(
        jnp.bfloat16
    )
    raw = jnp.concatenate(outputs, axis=0) + jnp.einsum(
        "thd,hde->the", scaled, incoming.astype(jnp.bfloat16), preferred_element_type=jnp.float32
    )
    square_mean = jnp.mean(raw * raw, axis=2, keepdims=True)
    normed = raw * lax.rsqrt(square_mean + EPS) * norm_gain.reshape(heads, width)
    return normed.astype(jnp.bfloat16).reshape(length, columns), held


def attend(query_blk, keys_sel, values_sel, allowed):
    width = query_blk.shape[-1]
    inverse_root = 1.0 / math.sqrt(width)
    scores = (
        jnp.einsum("thd,kjhd->htkj", query_blk, keys_sel, preferred_element_type=jnp.float32)
        * inverse_root
    )
    scores = jnp.where(allowed[None], scores, -jnp.inf)
    highest = jnp.max(scores, axis=(2, 3), keepdims=True)
    raised = jnp.exp(scores - highest)
    weights = (raised / jnp.sum(raised, axis=(2, 3), keepdims=True)).astype(jnp.bfloat16)
    output = jnp.einsum("htkj,kjhd->thd", weights, values_sel, preferred_element_type=jnp.float32)
    return output.astype(jnp.bfloat16)


def softmax_layer(soft_query, soft_key, soft_value, block_index, block_count, heads, sections):
    length, columns = soft_query.shape
    per_section = length // BLK
    slots = block_index.shape[1]
    own_pair = (soft_key, soft_value)
    farther = passed_along(own_pair, CTX, 2, sections)
    on_first = lax.axis_index("cc") == 0
    handed = jax.tree.map(lambda own, far: jnp.where(on_first, own, far), own_pair, farther)
    nearer = swapped(handed)
    pieces = [farther, nearer]
    window_key = jnp.concatenate([piece[0] for piece in pieces] + [soft_key], axis=0)
    window_value = jnp.concatenate([piece[1] for piece in pieces] + [soft_value], axis=0)
    key_blocks = to_blocks(window_key, heads)
    value_blocks = to_blocks(window_value, heads)
    section = lax.axis_index(CTX)
    first_block = (section - WIN_SEC) * per_section
    query_blocks = to_blocks(soft_query, heads)
    causal = causal_mask(BLK)
    slot_ids = jnp.arange(slots, dtype=jnp.int32)
    outputs = []
    for b in range(per_section):
        row_global = section * per_section + b
        low = b + WIN_SEC * per_section - (slots - 1)
        candidates = first_block + low + jnp.arange(slots, dtype=jnp.int32)
        used = slot_ids < block_count[b]
        matches = (block_index[b][None, :] == candidates[:, None]) & used[None, :]
        named = jnp.any(matches, axis=1)
        off_diagonal = candidates != row_global
        allowed = named[None, :, None] & (off_diagonal[None, :, None] | causal[:, None, :])
        outputs.append(
            attend(
                query_blocks[b],
                key_blocks[low : low + slots],
                value_blocks[low : low + slots],
                allowed,
            )
        )
    return jnp.concatenate(outputs, axis=0).reshape(length, columns)


def local(
    linear_query,
    linear_key,
    linear_value,
    log_decay,
    norm_gain,
    soft_query,
    soft_key,
    soft_value,
    block_index,
    block_count,
):
    heads = log_decay.shape[0]
    sections = lax.psum(1, CTX)
    softmax_heads = softmax_layer(
        soft_query, soft_key, soft_value, block_index, block_count, heads, sections
    )
    softmax_rows = lax.all_to_all(softmax_heads, "head", split_axis=0, concat_axis=1, tiled=True)
    linear_heads, softmax_rows = linear_layer(
        linear_query, linear_key, linear_value, log_decay, norm_gain, softmax_rows
    )
    linear_rows = lax.all_to_all(linear_heads, "head", split_axis=0, concat_axis=1, tiled=True)
    return (linear_rows, softmax_rows)


def solution(mesh):
    ctx, head = mesh.devices.shape
    split = mesh.devices.reshape(ctx // 16, 8, 2, head)
    mesh = jax.sharding.Mesh(split, CTX + ("head",))
    rows = P(CTX, "head")
    in_specs = (
        rows,
        rows,
        rows,
        P("head", CTX),
        P("head"),
        rows,
        rows,
        rows,
        P(CTX, None),
        P(CTX),
    )
    out_specs = (P(CTX + ("head",), None), P(CTX + ("head",), None))
    return jax.shard_map(local, mesh=mesh, in_specs=in_specs, out_specs=out_specs, check_vma=False)
```

```python
import math

import jax
import jax.numpy as jnp
from jax import lax
from jax.sharding import PartitionSpec as P

BLK = 128
WIN_SEC = 2


EPS = 1e-06


CTX = ("cy", "cz", "cc")


def passed_along(block, axis, distance, count):
    devices = range(count)
    route = [(i - distance, i) for i in devices if i - distance in devices]
    return lax.ppermute(block, axis, route)


def causal_mask(length):
    rows_iota = lax.broadcasted_iota(jnp.int32, (length, length), 0)
    cols_iota = lax.broadcasted_iota(jnp.int32, (length, length), 1)
    return cols_iota <= rows_iota


def to_blocks(matrix, heads):
    length, columns = matrix.shape
    return matrix.reshape(length // BLK, BLK, heads, columns // heads)


def block_state(carried, keys_blk, values_blk, cumul_blk, total_blk):
    factor = jnp.exp(total_blk[:, None] - cumul_blk).T
    decayed = (keys_blk.astype(jnp.float32) * factor[:, :, None]).astype(jnp.bfloat16)
    update = jnp.einsum("jhd,jhe->hde", decayed, values_blk, preferred_element_type=jnp.float32)
    return jnp.exp(total_blk)[:, None, None] * carried + update


def block_output(carried, query_blk, keys_blk, values_blk, cumul_blk):
    scores = jnp.einsum("thd,jhd->htj", query_blk, keys_blk, preferred_element_type=jnp.float32)
    differ = cumul_blk[:, :, None] - cumul_blk[:, None, :]
    allowed = causal_mask(query_blk.shape[0])
    weights = jnp.where(allowed[None], jnp.exp(jnp.minimum(differ, 0.0)), 0.0)
    mixing = (scores * weights).astype(jnp.bfloat16)
    inside = jnp.einsum("htj,jhd->thd", mixing, values_blk, preferred_element_type=jnp.float32)
    decayed_query = (query_blk.astype(jnp.float32) * jnp.exp(cumul_blk).T[:, :, None]).astype(
        jnp.bfloat16
    )
    across = jnp.einsum(
        "thd,hde->the",
        decayed_query,
        carried.astype(jnp.bfloat16),
        preferred_element_type=jnp.float32,
    )
    return inside + across


def packed(state, factor):
    heads, width, _ = state.shape
    return jnp.concatenate([state, jnp.broadcast_to(factor[:, None, None], (heads, 8, width))], axis=1)


def unpacked(both, width):
    return both[..., :width, :], both[..., width, 0]


def narrow(state, factor):
    heads, width, _ = state.shape
    high = factor.astype(jnp.bfloat16)
    low = (factor - high.astype(jnp.float32)).astype(jnp.bfloat16)
    rows = lambda part: jnp.broadcast_to(part[:, None, None], (heads, 8, width))
    return jnp.concatenate([state.astype(jnp.bfloat16), rows(high), rows(low)], axis=1)


def widened(both, width):
    wide = both.astype(jnp.float32)
    return wide[..., :width, :], wide[..., width, 0] + wide[..., width + 8, 0]


def folding_weights(factors, upto):
    places = jnp.arange(factors.shape[0])
    between = (places[:, None] < places[None, :]) & (places[None, :] < upto)
    weights = jnp.prod(jnp.where(between[:, :, None], factors[None], 1.0), axis=1)
    return jnp.where((places < upto)[:, None], weights, 0.0)


def folded(states, factors, upto):
    weights = folding_weights(factors, upto)
    return jnp.sum(weights[:, :, None, None] * states, axis=0)


def spanned(factors, upto):
    places = jnp.arange(factors.shape[0])
    return jnp.prod(jnp.where((places < upto)[:, None], factors, 1.0), axis=0)


def swapped(block):
    return lax.ppermute(block, "cc", [(0, 1), (1, 0)])


def carry_in(final, section_total, held):
    heads, width, _ = final.shape
    half = heads // 2
    core, row, column = (lax.axis_index("cc"), lax.axis_index("cz"), lax.axis_index("cy"))
    factor = jnp.exp(section_total)
    other_state, other_factor = unpacked(swapped(packed(final, factor)), width)
    on_first = core == 0
    first_state = jnp.where(on_first, final, other_state)
    first_all = jnp.where(on_first, factor, other_factor)
    second_state = jnp.where(on_first, other_state, final)
    second_all = jnp.where(on_first, other_factor, factor)
    low = core * half
    first = lax.dynamic_slice_in_dim(first_state, low, half, 0)
    second = lax.dynamic_slice_in_dim(second_state, low, half, 0)
    first_factor = lax.dynamic_slice_in_dim(first_all, low, half, 0)
    second_factor = lax.dynamic_slice_in_dim(second_all, low, half, 0)
    chip_state = second_factor[:, None, None] * first + second
    chip_factor = first_factor * second_factor
    row_states, row_factors = widened(
        lax.all_gather(narrow(chip_state, chip_factor), "cz"), width
    )
    count = row_states.shape[0]
    before = folded(row_states, row_factors, row)
    before_factor = spanned(row_factors, row)
    total = folded(row_states, row_factors, count)
    total_factor = spanned(row_factors, count)
    mine = packed(total, total_factor)
    columns = lax.psum(1, "cy")
    received = [
        lax.ppermute(mine, "cy", [(i, i + d) for i in range(columns) if i + d < columns])
        for d in range(columns - 1, 0, -1)
    ]
    received, held = lax.optimization_barrier((received, held))
    parts = [unpacked(piece, width) for piece in received]
    weights = folding_weights(jnp.stack([part[1] for part in parts]), columns - 1)
    above = sum(weight[:, None, None] * part[0] for weight, part in zip(weights, parts))
    prefix_half = before_factor[:, None, None] * above + before
    other_half = swapped(prefix_half)
    prefix = jnp.where(
        on_first,
        jnp.concatenate([prefix_half, other_half], axis=0),
        jnp.concatenate([other_half, prefix_half], axis=0),
    )
    later = first_all[:, None, None] * prefix + first_state
    return jnp.where(on_first, prefix, later), held


def linear_layer(linear_query, linear_key, linear_value, log_decay, norm_gain, held):
    length, columns = linear_query.shape
    heads = log_decay.shape[0]
    width = columns // heads
    blocks_here = length // BLK
    query_blocks = to_blocks(linear_query, heads)
    keys_blocks = to_blocks(linear_key, heads)
    values_blocks = to_blocks(linear_value, heads)
    per_block = log_decay.reshape(heads, blocks_here, BLK).transpose(1, 0, 2)
    cumulative = jnp.cumsum(per_block, axis=2)
    totals = cumulative[:, :, -1]
    section_cum = jnp.cumsum(log_decay, axis=1)
    section_total = section_cum[:, -1]
    carried = jnp.zeros((heads, width, width), jnp.float32)
    before = []
    for b in range(blocks_here):
        before.append(carried)
        carried = block_state(carried, keys_blocks[b], values_blocks[b], cumulative[b], totals[b])
    incoming, held = carry_in(carried, section_total, held)
    outputs = [
        block_output(before[b], query_blocks[b], keys_blocks[b], values_blocks[b], cumulative[b])
        for b in range(blocks_here)
    ]
    queries_flat = linear_query.reshape(length, heads, width)
    scaled = (queries_flat.astype(jnp.float32) * jnp.exp(section_cum).T[:, :, None]).astype(
        jnp.bfloat16
    )
    raw = jnp.concatenate(outputs, axis=0) + jnp.einsum(
        "thd,hde->the", scaled, incoming.astype(jnp.bfloat16), preferred_element_type=jnp.float32
    )
    square_mean = jnp.mean(raw * raw, axis=2, keepdims=True)
    normed = raw * lax.rsqrt(square_mean + EPS) * norm_gain.reshape(heads, width)
    return normed.astype(jnp.bfloat16).reshape(length, columns), held


def attend(query_blk, keys_sel, values_sel, allowed):
    width = query_blk.shape[-1]
    inverse_root = 1.0 / math.sqrt(width)
    scores = (
        jnp.einsum("thd,kjhd->htkj", query_blk, keys_sel, preferred_element_type=jnp.float32)
        * inverse_root
    )
    scores = jnp.where(allowed[None], scores, -jnp.inf)
    highest = jnp.max(scores, axis=(2, 3), keepdims=True)
    raised = jnp.exp(scores - highest)
    weights = (raised / jnp.sum(raised, axis=(2, 3), keepdims=True)).astype(jnp.bfloat16)
    output = jnp.einsum("htkj,kjhd->thd", weights, values_sel, preferred_element_type=jnp.float32)
    return output.astype(jnp.bfloat16)


def softmax_layer(soft_query, soft_key, soft_value, block_index, block_count, heads, sections):
    length, columns = soft_query.shape
    per_section = length // BLK
    slots = block_index.shape[1]
    own_pair = (soft_key, soft_value)
    farther = passed_along(own_pair, CTX, 2, sections)
    on_first = lax.axis_index("cc") == 0
    handed = jax.tree.map(lambda own, far: jnp.where(on_first, own, far), own_pair, farther)
    nearer = swapped(handed)
    pieces = [farther, nearer]
    window_key = jnp.concatenate([piece[0] for piece in pieces] + [soft_key], axis=0)
    window_value = jnp.concatenate([piece[1] for piece in pieces] + [soft_value], axis=0)
    key_blocks = to_blocks(window_key, heads)
    value_blocks = to_blocks(window_value, heads)
    section = lax.axis_index(CTX)
    first_block = (section - WIN_SEC) * per_section
    query_blocks = to_blocks(soft_query, heads)
    causal = causal_mask(BLK)
    slot_ids = jnp.arange(slots, dtype=jnp.int32)
    outputs = []
    for b in range(per_section):
        row_global = section * per_section + b
        low = b + WIN_SEC * per_section - (slots - 1)
        candidates = first_block + low + jnp.arange(slots, dtype=jnp.int32)
        used = slot_ids < block_count[b]
        matches = (block_index[b][None, :] == candidates[:, None]) & used[None, :]
        named = jnp.any(matches, axis=1)
        off_diagonal = candidates != row_global
        allowed = named[None, :, None] & (off_diagonal[None, :, None] | causal[:, None, :])
        outputs.append(
            attend(
                query_blocks[b],
                key_blocks[low : low + slots],
                value_blocks[low : low + slots],
                allowed,
            )
        )
    return jnp.concatenate(outputs, axis=0).reshape(length, columns)


def local(
    linear_query,
    linear_key,
    linear_value,
    log_decay,
    norm_gain,
    soft_query,
    soft_key,
    soft_value,
    block_index,
    block_count,
):
    heads = log_decay.shape[0]
    sections = lax.psum(1, CTX)
    softmax_heads = softmax_layer(
        soft_query, soft_key, soft_value, block_index, block_count, heads, sections
    )
    softmax_rows = lax.all_to_all(softmax_heads, "head", split_axis=0, concat_axis=1, tiled=True)
    linear_heads, softmax_rows = linear_layer(
        linear_query, linear_key, linear_value, log_decay, norm_gain, softmax_rows
    )
    linear_rows = lax.all_to_all(linear_heads, "head", split_axis=0, concat_axis=1, tiled=True)
    return (linear_rows, softmax_rows)


def solution(mesh):
    ctx, head = mesh.devices.shape
    split = mesh.devices.reshape(ctx // 16, 8, 2, head)
    mesh = jax.sharding.Mesh(split, CTX + ("head",))
    rows = P(CTX, "head")
    in_specs = (
        rows,
        rows,
        rows,
        P("head", CTX),
        P("head"),
        rows,
        rows,
        rows,
        P(CTX, None),
        P(CTX),
    )
    out_specs = (P(CTX + ("head",), None), P(CTX + ("head",), None))
    return jax.shard_map(local, mesh=mesh, in_specs=in_specs, out_specs=out_specs, check_vma=False)
```

```python
import math

import jax
import jax.numpy as jnp
from jax import lax
from jax.sharding import PartitionSpec as P

BLK = 128
WIN_SEC = 2


EPS = 1e-06


CTX = ("cy", "cz", "cc")


def passed_along(block, axis, distance, count):
    devices = range(count)
    route = [(i - distance, i) for i in devices if i - distance in devices]
    return lax.ppermute(block, axis, route)


def causal_mask(length):
    rows_iota = lax.broadcasted_iota(jnp.int32, (length, length), 0)
    cols_iota = lax.broadcasted_iota(jnp.int32, (length, length), 1)
    return cols_iota <= rows_iota


def to_blocks(matrix, heads):
    length, columns = matrix.shape
    return matrix.reshape(length // BLK, BLK, heads, columns // heads)


def block_state(carried, keys_blk, values_blk, cumul_blk, total_blk):
    factor = jnp.exp(total_blk[:, None] - cumul_blk).T
    decayed = (keys_blk.astype(jnp.float32) * factor[:, :, None]).astype(jnp.bfloat16)
    update = jnp.einsum("jhd,jhe->hde", decayed, values_blk, preferred_element_type=jnp.float32)
    return jnp.exp(total_blk)[:, None, None] * carried + update


def block_output(carried, query_blk, keys_blk, values_blk, cumul_blk):
    scores = jnp.einsum("thd,jhd->htj", query_blk, keys_blk, preferred_element_type=jnp.float32)
    differ = cumul_blk[:, :, None] - cumul_blk[:, None, :]
    allowed = causal_mask(query_blk.shape[0])
    weights = jnp.where(allowed[None], jnp.exp(jnp.minimum(differ, 0.0)), 0.0)
    mixing = (scores * weights).astype(jnp.bfloat16)
    inside = jnp.einsum("htj,jhd->thd", mixing, values_blk, preferred_element_type=jnp.float32)
    decayed_query = (query_blk.astype(jnp.float32) * jnp.exp(cumul_blk).T[:, :, None]).astype(
        jnp.bfloat16
    )
    across = jnp.einsum(
        "thd,hde->the",
        decayed_query,
        carried.astype(jnp.bfloat16),
        preferred_element_type=jnp.float32,
    )
    return inside + across


def packed(state, factor):
    heads, width, _ = state.shape
    return jnp.concatenate([state, jnp.broadcast_to(factor[:, None, None], (heads, 8, width))], axis=1)


def unpacked(both, width):
    return both[..., :width, :], both[..., width, 0]


def folding_weights(factors, upto):
    places = jnp.arange(factors.shape[0])
    between = (places[:, None] < places[None, :]) & (places[None, :] < upto)
    weights = jnp.prod(jnp.where(between[:, :, None], factors[None], 1.0), axis=1)
    return jnp.where((places < upto)[:, None], weights, 0.0)


def folded(states, factors, upto):
    weights = folding_weights(factors, upto)
    return jnp.sum(weights[:, :, None, None] * states, axis=0)


def spanned(factors, upto):
    places = jnp.arange(factors.shape[0])
    return jnp.prod(jnp.where((places < upto)[:, None], factors, 1.0), axis=0)


def swapped(block):
    return lax.ppermute(block, "cc", [(0, 1), (1, 0)])


def carry_in(final, section_total, held):
    heads, width, _ = final.shape
    half = heads // 2
    core, row, column = (lax.axis_index("cc"), lax.axis_index("cz"), lax.axis_index("cy"))
    factor = jnp.exp(section_total)
    other_state, other_factor = unpacked(swapped(packed(final, factor)), width)
    on_first = core == 0
    first_state = jnp.where(on_first, final, other_state)
    first_all = jnp.where(on_first, factor, other_factor)
    second_state = jnp.where(on_first, other_state, final)
    second_all = jnp.where(on_first, other_factor, factor)
    low = core * half
    first = lax.dynamic_slice_in_dim(first_state, low, half, 0)
    second = lax.dynamic_slice_in_dim(second_state, low, half, 0)
    first_factor = lax.dynamic_slice_in_dim(first_all, low, half, 0)
    second_factor = lax.dynamic_slice_in_dim(second_all, low, half, 0)
    chip_state = second_factor[:, None, None] * first + second
    chip_factor = first_factor * second_factor
    row_states, row_factors = unpacked(
        lax.all_gather(packed(chip_state, chip_factor), "cz"), width
    )
    count = row_states.shape[0]
    before = folded(row_states, row_factors, row)
    before_factor = spanned(row_factors, row)
    total = folded(row_states, row_factors, count)
    total_factor = spanned(row_factors, count)
    mine = packed(total, total_factor)
    columns = lax.psum(1, "cy")
    received = [
        lax.ppermute(mine, "cy", [(i, i + d) for i in range(columns) if i + d < columns])
        for d in range(columns - 1, 0, -1)
    ]
    received, held = lax.optimization_barrier((received, held))
    parts = [unpacked(piece, width) for piece in received]
    weights = folding_weights(jnp.stack([part[1] for part in parts]), columns - 1)
    above = sum(weight[:, None, None] * part[0] for weight, part in zip(weights, parts))
    prefix_half = before_factor[:, None, None] * above + before
    other_half = swapped(prefix_half)
    prefix = jnp.where(
        on_first,
        jnp.concatenate([prefix_half, other_half], axis=0),
        jnp.concatenate([other_half, prefix_half], axis=0),
    )
    later = first_all[:, None, None] * prefix + first_state
    return jnp.where(on_first, prefix, later), held


def linear_layer(linear_query, linear_key, linear_value, log_decay, norm_gain, held):
    length, columns = linear_query.shape
    heads = log_decay.shape[0]
    width = columns // heads
    blocks_here = length // BLK
    query_blocks = to_blocks(linear_query, heads)
    keys_blocks = to_blocks(linear_key, heads)
    values_blocks = to_blocks(linear_value, heads)
    per_block = log_decay.reshape(heads, blocks_here, BLK).transpose(1, 0, 2)
    cumulative = jnp.cumsum(per_block, axis=2)
    totals = cumulative[:, :, -1]
    section_cum = jnp.cumsum(log_decay, axis=1)
    section_total = section_cum[:, -1]
    carried = jnp.zeros((heads, width, width), jnp.float32)
    before = []
    for b in range(blocks_here):
        before.append(carried)
        carried = block_state(carried, keys_blocks[b], values_blocks[b], cumulative[b], totals[b])
    incoming, held = carry_in(carried, section_total, held)
    outputs = [
        block_output(before[b], query_blocks[b], keys_blocks[b], values_blocks[b], cumulative[b])
        for b in range(blocks_here)
    ]
    queries_flat = linear_query.reshape(length, heads, width)
    scaled = (queries_flat.astype(jnp.float32) * jnp.exp(section_cum).T[:, :, None]).astype(
        jnp.bfloat16
    )
    raw = jnp.concatenate(outputs, axis=0) + jnp.einsum(
        "thd,hde->the", scaled, incoming.astype(jnp.bfloat16), preferred_element_type=jnp.float32
    )
    square_mean = jnp.mean(raw * raw, axis=2, keepdims=True)
    normed = raw * lax.rsqrt(square_mean + EPS) * norm_gain.reshape(heads, width)
    return normed.astype(jnp.bfloat16).reshape(length, columns), held


def attend(query_blk, keys_sel, values_sel, allowed):
    width = query_blk.shape[-1]
    inverse_root = 1.0 / math.sqrt(width)
    scores = (
        jnp.einsum("thd,kjhd->htkj", query_blk, keys_sel, preferred_element_type=jnp.float32)
        * inverse_root
    )
    scores = jnp.where(allowed[None], scores, -jnp.inf)
    highest = jnp.max(scores, axis=(2, 3), keepdims=True)
    raised = jnp.exp(scores - highest)
    weights = (raised / jnp.sum(raised, axis=(2, 3), keepdims=True)).astype(jnp.bfloat16)
    output = jnp.einsum("htkj,kjhd->thd", weights, values_sel, preferred_element_type=jnp.float32)
    return output.astype(jnp.bfloat16)


def softmax_layer(soft_query, soft_key, soft_value, block_index, block_count, heads, sections):
    length, columns = soft_query.shape
    per_section = length // BLK
    slots = block_index.shape[1]
    own_pair = (soft_key, soft_value)
    farther = passed_along(own_pair, CTX, 2, sections)
    on_first = lax.axis_index("cc") == 0
    handed = jax.tree.map(lambda own, far: jnp.where(on_first, own, far), own_pair, farther)
    nearer = swapped(handed)
    pieces = [farther, nearer]
    window_key = jnp.concatenate([piece[0] for piece in pieces] + [soft_key], axis=0)
    window_value = jnp.concatenate([piece[1] for piece in pieces] + [soft_value], axis=0)
    key_blocks = to_blocks(window_key, heads)
    value_blocks = to_blocks(window_value, heads)
    section = lax.axis_index(CTX)
    first_block = (section - WIN_SEC) * per_section
    query_blocks = to_blocks(soft_query, heads)
    causal = causal_mask(BLK)
    slot_ids = jnp.arange(slots, dtype=jnp.int32)
    outputs = []
    for b in range(per_section):
        row_global = section * per_section + b
        low = b + WIN_SEC * per_section - (slots - 1)
        candidates = first_block + low + jnp.arange(slots, dtype=jnp.int32)
        used = slot_ids < block_count[b]
        matches = (block_index[b][None, :] == candidates[:, None]) & used[None, :]
        named = jnp.any(matches, axis=1)
        off_diagonal = candidates != row_global
        allowed = named[None, :, None] & (off_diagonal[None, :, None] | causal[:, None, :])
        outputs.append(
            attend(
                query_blocks[b],
                key_blocks[low : low + slots],
                value_blocks[low : low + slots],
                allowed,
            )
        )
    return jnp.concatenate(outputs, axis=0).reshape(length, columns)


def local(
    linear_query,
    linear_key,
    linear_value,
    log_decay,
    norm_gain,
    soft_query,
    soft_key,
    soft_value,
    block_index,
    block_count,
):
    heads = log_decay.shape[0]
    sections = lax.psum(1, CTX)
    softmax_heads = softmax_layer(
        soft_query, soft_key, soft_value, block_index, block_count, heads, sections
    )
    softmax_rows = lax.all_to_all(softmax_heads, "head", split_axis=0, concat_axis=1, tiled=True)
    linear_heads, softmax_rows = linear_layer(
        linear_query, linear_key, linear_value, log_decay, norm_gain, softmax_rows
    )
    linear_rows = lax.all_to_all(linear_heads, "head", split_axis=0, concat_axis=1, tiled=True)
    return (linear_rows, softmax_rows)


def solution(mesh):
    ctx, head = mesh.devices.shape
    split = mesh.devices.reshape(ctx // 16, 8, 2, head)
    mesh = jax.sharding.Mesh(split, CTX + ("head",))
    rows = P(CTX, "head")
    in_specs = (
        rows,
        rows,
        rows,
        P("head", CTX),
        P("head"),
        rows,
        rows,
        rows,
        P(CTX, None),
        P(CTX),
    )
    out_specs = (P(CTX + ("head",), None), P(CTX + ("head",), None))
    return jax.shard_map(local, mesh=mesh, in_specs=in_specs, out_specs=out_specs, check_vma=False)
```

```python
import math

import jax
import jax.numpy as jnp
from jax import lax
from jax.sharding import PartitionSpec as P

BLK = 128
WIN_SEC = 2


EPS = 1e-06


CTX = ("cy", "cz", "cc")


def passed_along(block, axis, distance, count):
    devices = range(count)
    route = [(i - distance, i) for i in devices if i - distance in devices]
    return lax.ppermute(block, axis, route)


def causal_mask(length):
    rows_iota = lax.broadcasted_iota(jnp.int32, (length, length), 0)
    cols_iota = lax.broadcasted_iota(jnp.int32, (length, length), 1)
    return cols_iota <= rows_iota


def to_blocks(matrix, heads):
    length, columns = matrix.shape
    return matrix.reshape(length // BLK, BLK, heads, columns // heads)


def block_state(carried, keys_blk, values_blk, cumul_blk, total_blk):
    factor = jnp.exp(total_blk[:, None] - cumul_blk).T
    decayed = (keys_blk.astype(jnp.float32) * factor[:, :, None]).astype(jnp.bfloat16)
    update = jnp.einsum("jhd,jhe->hde", decayed, values_blk, preferred_element_type=jnp.float32)
    return jnp.exp(total_blk)[:, None, None] * carried + update


def block_output(carried, query_blk, keys_blk, values_blk, cumul_blk):
    scores = jnp.einsum("thd,jhd->htj", query_blk, keys_blk, preferred_element_type=jnp.float32)
    differ = cumul_blk[:, :, None] - cumul_blk[:, None, :]
    allowed = causal_mask(query_blk.shape[0])
    weights = jnp.where(allowed[None], jnp.exp(jnp.minimum(differ, 0.0)), 0.0)
    mixing = (scores * weights).astype(jnp.bfloat16)
    inside = jnp.einsum("htj,jhd->thd", mixing, values_blk, preferred_element_type=jnp.float32)
    decayed_query = (query_blk.astype(jnp.float32) * jnp.exp(cumul_blk).T[:, :, None]).astype(
        jnp.bfloat16
    )
    across = jnp.einsum(
        "thd,hde->the",
        decayed_query,
        carried.astype(jnp.bfloat16),
        preferred_element_type=jnp.float32,
    )
    return inside + across


def packed(state, factor):
    heads, width, _ = state.shape
    return jnp.concatenate([state, jnp.broadcast_to(factor[:, None, None], (heads, 8, width))], axis=1)


def unpacked(both, width):
    return both[..., :width, :], both[..., width, 0]


def folding_weights(factors, upto):
    places = jnp.arange(factors.shape[0])
    between = (places[:, None] < places[None, :]) & (places[None, :] < upto)
    weights = jnp.prod(jnp.where(between[:, :, None], factors[None], 1.0), axis=1)
    return jnp.where((places < upto)[:, None], weights, 0.0)


def folded(states, factors, upto):
    weights = folding_weights(factors, upto)
    return jnp.sum(weights[:, :, None, None] * states, axis=0)


def spanned(factors, upto):
    places = jnp.arange(factors.shape[0])
    return jnp.prod(jnp.where((places < upto)[:, None], factors, 1.0), axis=0)


def swapped(block):
    return lax.ppermute(block, "cc", [(0, 1), (1, 0)])


def carry_in(final, section_total, held):
    heads, width, _ = final.shape
    half = heads // 2
    core, row, column = (lax.axis_index("cc"), lax.axis_index("cz"), lax.axis_index("cy"))
    factor = jnp.exp(section_total)
    other_state, other_factor = unpacked(swapped(packed(final, factor)), width)
    on_first = core == 0
    first_state = jnp.where(on_first, final, other_state)
    first_all = jnp.where(on_first, factor, other_factor)
    second_state = jnp.where(on_first, other_state, final)
    second_all = jnp.where(on_first, other_factor, factor)
    low = core * half
    first = lax.dynamic_slice_in_dim(first_state, low, half, 0)
    second = lax.dynamic_slice_in_dim(second_state, low, half, 0)
    first_factor = lax.dynamic_slice_in_dim(first_all, low, half, 0)
    second_factor = lax.dynamic_slice_in_dim(second_all, low, half, 0)
    chip_state = second_factor[:, None, None] * first + second
    chip_factor = first_factor * second_factor
    row_states, row_factors = unpacked(
        lax.all_gather(packed(chip_state, chip_factor), "cz"), width
    )
    count = row_states.shape[0]
    before = folded(row_states, row_factors, row)
    before_factor = spanned(row_factors, row)
    total = folded(row_states, row_factors, count)
    total_factor = spanned(row_factors, count)
    mine = packed(total, total_factor)
    columns = lax.psum(1, "cy")
    received = [
        lax.ppermute(mine, "cy", [(i, i + d) for i in range(columns) if i + d < columns])
        for d in range(columns - 1, 0, -1)
    ]
    received, held = lax.optimization_barrier((received, held))
    parts = [unpacked(piece, width) for piece in received]
    weights = folding_weights(jnp.stack([part[1] for part in parts]), columns - 1)
    above = sum(weight[:, None, None] * part[0] for weight, part in zip(weights, parts))
    prefix_half = before_factor[:, None, None] * above + before
    other_half = swapped(prefix_half)
    prefix = jnp.where(
        on_first,
        jnp.concatenate([prefix_half, other_half], axis=0),
        jnp.concatenate([other_half, prefix_half], axis=0),
    )
    later = first_all[:, None, None] * prefix + first_state
    return jnp.where(on_first, prefix, later), held


def linear_layer(linear_query, linear_key, linear_value, log_decay, norm_gain, held):
    length, columns = linear_query.shape
    heads = log_decay.shape[0]
    width = columns // heads
    blocks_here = length // BLK
    query_blocks = to_blocks(linear_query, heads)
    keys_blocks = to_blocks(linear_key, heads)
    values_blocks = to_blocks(linear_value, heads)
    per_block = log_decay.reshape(heads, blocks_here, BLK).transpose(1, 0, 2)
    cumulative = jnp.cumsum(per_block, axis=2)
    totals = cumulative[:, :, -1]
    section_cum = jnp.cumsum(log_decay, axis=1)
    section_total = section_cum[:, -1]
    carried = jnp.zeros((heads, width, width), jnp.float32)
    before = []
    for b in range(blocks_here):
        before.append(carried)
        carried = block_state(carried, keys_blocks[b], values_blocks[b], cumulative[b], totals[b])
    incoming, held = carry_in(carried, section_total, held)
    outputs = [
        block_output(before[b], query_blocks[b], keys_blocks[b], values_blocks[b], cumulative[b])
        for b in range(blocks_here)
    ]
    queries_flat = linear_query.reshape(length, heads, width)
    scaled = (queries_flat.astype(jnp.float32) * jnp.exp(section_cum).T[:, :, None]).astype(
        jnp.bfloat16
    )
    raw = jnp.concatenate(outputs, axis=0) + jnp.einsum(
        "thd,hde->the", scaled, incoming.astype(jnp.bfloat16), preferred_element_type=jnp.float32
    )
    square_mean = jnp.mean(raw * raw, axis=2, keepdims=True)
    normed = raw * lax.rsqrt(square_mean + EPS) * norm_gain.reshape(heads, width)
    return normed.astype(jnp.bfloat16).reshape(length, columns), held


def attend(query_blk, keys_sel, values_sel, allowed):
    width = query_blk.shape[-1]
    inverse_root = 1.0 / math.sqrt(width)
    scores = (
        jnp.einsum("thd,kjhd->htkj", query_blk, keys_sel, preferred_element_type=jnp.float32)
        * inverse_root
    )
    scores = jnp.where(allowed[None], scores, -jnp.inf)
    highest = jnp.max(scores, axis=(2, 3), keepdims=True)
    raised = jnp.exp(scores - highest)
    weights = (raised / jnp.sum(raised, axis=(2, 3), keepdims=True)).astype(jnp.bfloat16)
    output = jnp.einsum("htkj,kjhd->thd", weights, values_sel, preferred_element_type=jnp.float32)
    return output.astype(jnp.bfloat16)


def softmax_layer(soft_query, soft_key, soft_value, block_index, block_count, heads, sections):
    length, columns = soft_query.shape
    per_section = length // BLK
    slots = block_index.shape[1]
    own_pair = (soft_key, soft_value)
    farther = passed_along(own_pair, CTX, 2, sections)
    on_first = lax.axis_index("cc") == 0
    handed = jax.tree.map(lambda own, far: jnp.where(on_first, own, far), own_pair, farther)
    nearer = swapped(handed)
    pieces = [farther, nearer]
    window_key = jnp.concatenate([piece[0] for piece in pieces] + [soft_key], axis=0)
    window_value = jnp.concatenate([piece[1] for piece in pieces] + [soft_value], axis=0)
    key_blocks = to_blocks(window_key, heads)
    value_blocks = to_blocks(window_value, heads)
    section = lax.axis_index(CTX)
    first_block = (section - WIN_SEC) * per_section
    query_blocks = to_blocks(soft_query, heads)
    causal = causal_mask(BLK)
    slot_ids = jnp.arange(slots, dtype=jnp.int32)
    outputs = []
    for b in range(per_section):
        row_global = section * per_section + b
        low = b + WIN_SEC * per_section - (slots - 1)
        candidates = first_block + low + jnp.arange(slots, dtype=jnp.int32)
        used = slot_ids < block_count[b]
        matches = (block_index[b][None, :] == candidates[:, None]) & used[None, :]
        named = jnp.any(matches, axis=1)
        off_diagonal = candidates != row_global
        allowed = named[None, :, None] & (off_diagonal[None, :, None] | causal[:, None, :])
        outputs.append(
            attend(
                query_blocks[b],
                key_blocks[low : low + slots],
                value_blocks[low : low + slots],
                allowed,
            )
        )
    return jnp.concatenate(outputs, axis=0).reshape(length, columns)


def rows_by_permutes(block):
    count, mine = (lax.psum(1, "head"), lax.axis_index("head"))
    length, columns = block.shape
    share = length // count
    pieces = [lax.dynamic_slice_in_dim(block, mine * share, share, 0)]
    for d in range(1, count):
        outgoing = lax.dynamic_slice_in_dim(block, ((mine + d) % count) * share, share, 0)
        pieces.append(lax.ppermute(outgoing, "head", [(i, (i + d) % count) for i in range(count)]))
    ordered = jnp.roll(jnp.stack(pieces[::-1]), mine - (count - 1), axis=0)
    return ordered.transpose(1, 0, 2).reshape(share, count * columns)


def local(
    linear_query,
    linear_key,
    linear_value,
    log_decay,
    norm_gain,
    soft_query,
    soft_key,
    soft_value,
    block_index,
    block_count,
):
    heads = log_decay.shape[0]
    sections = lax.psum(1, CTX)
    softmax_heads = softmax_layer(
        soft_query, soft_key, soft_value, block_index, block_count, heads, sections
    )
    softmax_rows = lax.all_to_all(softmax_heads, "head", split_axis=0, concat_axis=1, tiled=True)
    linear_heads, softmax_rows = linear_layer(
        linear_query, linear_key, linear_value, log_decay, norm_gain, softmax_rows
    )
    linear_rows = rows_by_permutes(linear_heads)
    return (linear_rows, softmax_rows)


def solution(mesh):
    ctx, head = mesh.devices.shape
    split = mesh.devices.reshape(ctx // 16, 8, 2, head)
    mesh = jax.sharding.Mesh(split, CTX + ("head",))
    rows = P(CTX, "head")
    in_specs = (
        rows,
        rows,
        rows,
        P("head", CTX),
        P("head"),
        rows,
        rows,
        rows,
        P(CTX, None),
        P(CTX),
    )
    out_specs = (P(CTX + ("head",), None), P(CTX + ("head",), None))
    return jax.shard_map(local, mesh=mesh, in_specs=in_specs, out_specs=out_specs, check_vma=False)
```
